32 devices in a mesh: tm: 4 (over z), row: 4 (over y, x), col: 2 (over core).
Axes of the slice: x: 2, y: 2, z: 4, core: 2. Of those that a mesh axis runs over, the one named last changes fastest.
Arguments:
- reflectance: bfloat16 [32, 12, 128, 512], P('tm', None, 'row', 'col'), may hold values from -6 to 6
- scene_class: int32 [32, 128, 512], P('tm', 'row', 'col'), may hold values from 0 to 11
- quality: float32 [32, 128, 512], P('tm', 'row', 'col'), may hold values from -8 to 304
- class_score: float32 [12], replicated, may hold values from -4 to 2
- encode_first: bfloat16 [3, 3, 32, 12], replicated, may hold values from -0.875 to 0.875
- encode_second: bfloat16 [3, 3, 32, 32], replicated, may hold values from -0.5 to 0.5
- middle_first: bfloat16 [3, 3, 64, 32], replicated, may hold values from -0.5 to 0.5
- middle_second: bfloat16 [3, 3, 64, 64], replicated, may hold values from -0.375 to 0.375
- decode_kernel: bfloat16 [3, 3, 32, 96], replicated, may hold values from -0.3125 to 0.3125
- head_weight: bfloat16 [11, 32], replicated, may hold values from -1.5 to 1.5
Outputs:
- logits: bfloat16 [11, 128, 512], P(None, 'row', 'col')
The draws below stay inside these ranges and needn't reach their ends.
All inputs are finite; a program needn't handle non-finite values.
Results may differ from the reference program's by a relative error of at most 0.03.
Values may be sent and summed in bfloat16 or wider, within the bound.
No kernel may reach another device: no remote copies, remote signals or barrier semaphores. Data moves between devices by JAX's collectives and lax.ppermute only.
A program may use at most 64 MiB of HBM per device.

```python
import jax
import jax.numpy as jnp
from jax import lax

BANDS = 12
MASKCLS = 12
C0 = 32
C1 = 64
NCLS = 11
DATES = 32
NH = 128
NW = 512


def draw_quality(key, part):
    first_key = jax.random.fold_in(jax.random.fold_in(key, 17), 0)
    shape = (DATES, NH, NW)
    return jnp.clip(2.0 * jax.random.normal(first_key, shape, jnp.float32), -8.0, 8.0)


def with_ends(values, key, low, largest):
    extent = values.shape
    index_at = [jax.random.randint(jax.random.fold_in(key, axis), (), 0, extent[axis]) for axis in range(len(extent))]
    values = values.at[tuple(index_at)].set(low)
    longest = extent.index(max(extent))
    index_at[longest] = (index_at[longest] + 1) % extent[longest]
    return values.at[tuple(index_at)].set(largest)


def shard_levels(stream_key, dims, cuts, smallest, high):
    def one(dim, blocks):
        draws = jax.random.uniform(jax.random.fold_in(jax.random.fold_in(stream_key, 6), dim), (blocks,), jnp.float32, smallest / len(cuts), high / len(cuts))
        return jnp.repeat(jnp.exp(draws), dims[dim] // blocks).reshape((-1,) + (1,) * (len(dims) - dim - 1))

    gain = one(*cuts[0])
    for cut in cuts[1:]:
        gain = gain * one(*cut)
    return gain


def noise(own_key, extent, spread, most, pieces=(), held_as=jnp.bfloat16):
    drawn = jax.random.normal(own_key, extent, jnp.float32) * spread
    if len(pieces) > 0:
        drawn = shard_levels(own_key, extent, pieces, -0.22, 0.18) * drawn
    return jnp.clip(drawn, min=-most, max=most).astype(held_as)


def setup_inputs(seed: int = 0) -> dict:
    key_of = jax.random.split(jax.random.key(seed), 11)
    reflectance = noise(key_of[0], (DATES, BANDS, NH, NW), 1.0, 6.0, ((0, 4), (2, 4), (3, 2)))
    scene_class = with_ends(jax.random.randint(key_of[1], (DATES, NH, NW), 0, MASKCLS), jax.random.fold_in(key_of[1], 1), 0, MASKCLS - 1).astype(jnp.int32)
    quality = draw_quality(jax.random.fold_in(key_of[10], 71), 0)
    class_score = jnp.clip(jax.random.uniform(key_of[3], (MASKCLS,), jnp.float32, -4.0, 2.0), -4.0, 2.0)
    encode_first = noise(key_of[4], (3, 3, C0, BANDS), (9 * BANDS // 2) ** -0.5, 0.875)
    encode_second = noise(key_of[5], (3, 3, C0, C0), (9 * C0 // 2) ** -0.5, 0.5)
    middle_first = noise(key_of[6], (3, 3, C1, C0), (9 * C0 // 2) ** -0.5, 0.5)
    middle_second = noise(key_of[7], (3, 3, C1, C1), (9 * C1 // 2) ** -0.5, 0.375)
    decode_kernel = noise(key_of[8], (3, 3, C0, C0 + C1), (9 * (C0 + C1) // 2) ** -0.5, 0.3125)
    head_weight = noise(key_of[9], (NCLS, C0), (C0 // 2) ** -0.5, 1.5)
    return dict(reflectance=reflectance, scene_class=scene_class, quality=quality, class_score=class_score, encode_first=encode_first, encode_second=encode_second, middle_first=middle_first, middle_second=middle_second, decode_kernel=decode_kernel, head_weight=head_weight)


def convolve(field, kernel):
    return lax.conv_general_dilated(field[None], kernel, (1, 1), ((1, 1), (1, 1)), dimension_numbers=("NCHW", "HWOI", "NCHW"), preferred_element_type=jnp.float32)[0]


def relu_layer(field, kernel):
    return jnp.maximum(convolve(field, kernel), 0.0).astype(jnp.bfloat16)


def reference(reflectance, scene_class, quality, class_score, encode_first, encode_second, middle_first, middle_second, decode_kernel, head_weight):
    scores = class_score[scene_class] + quality
    top_score = jnp.max(scores, axis=0)
    weights = jnp.exp(scores - top_score[None])
    total_weight = jnp.sum(weights, axis=0)

    def accumulate(total, inputs):
        weight_now, bands_now = inputs
        return total + weight_now[None] * bands_now.astype(jnp.float32), None

    band_sums, unused = lax.scan(accumulate, jnp.zeros((BANDS, NH, NW), jnp.float32), (weights, reflectance))
    composite = (band_sums / total_weight[None]).astype(jnp.bfloat16)
    skip = relu_layer(relu_layer(composite, encode_first), encode_second)
    pooled = jnp.mean(skip.astype(jnp.float32).reshape(C0, NH // 2, 2, NW // 2, 2), axis=(2, 4)).astype(jnp.bfloat16)
    deeper = relu_layer(relu_layer(pooled, middle_first), middle_second)
    upsampled = jnp.repeat(jnp.repeat(deeper, 2, axis=1), 2, axis=2)
    joined = jnp.concatenate([skip, upsampled], axis=0)
    decoded = relu_layer(joined, decode_kernel)
    result = jnp.einsum("oc,chw->ohw", head_weight.astype(jnp.float32), decoded.astype(jnp.float32))
    return result.astype(jnp.bfloat16)
```

```python
import jax
import jax.numpy as jnp
from jax import lax
from jax.sharding import PartitionSpec as P

HALO = 8


def with_halo(cells, sides, width):
    for axis, dim in sides:
        count = lax.axis_size(axis)
        ends = count - 1
        head = lax.slice_in_dim(cells, 0, width, axis=dim)
        tail = lax.slice_in_dim(cells, cells.shape[dim] - width, cells.shape[dim], axis=dim)
        cells = jnp.concatenate(
            [
                lax.ppermute(tail, axis, [(i, (i + 1) % count) for i in range(ends)]),
                cells,
                lax.ppermute(head, axis, [((i + 1) % count, i) for i in range(ends)]),
            ],
            axis=dim,
        )
    return cells


def valid_conv(padded, kernel):
    return lax.conv_general_dilated(
        padded[None],
        kernel,
        (1, 1),
        "VALID",
        dimension_numbers=("NCHW", "HWOI", "NCHW"),
        preferred_element_type=jnp.float32,
    )[0]


def inside_mask(row_start, col_start, height, width, total_rows, total_cols):
    rows = row_start + jnp.arange(height, dtype=jnp.int32)
    cols = col_start + jnp.arange(width, dtype=jnp.int32)
    row_in = (rows >= 0) & (rows < total_rows)
    col_in = (cols >= 0) & (cols < total_cols)
    return (row_in[:, None] & col_in[None, :])[None]


def masked_layer(field, kernel, row_start, col_start, total_rows, total_cols):
    out = valid_conv(field, kernel)
    mask = inside_mask(row_start, col_start, out.shape[1], out.shape[2], total_rows, total_cols)
    return jnp.where(mask, jnp.maximum(out, 0.0), 0.0).astype(jnp.bfloat16)


def shards(
    reflectance,
    scene_class,
    quality,
    class_score,
    encode_first,
    encode_second,
    middle_first,
    middle_second,
    decode_kernel,
    head_weight,
):
    block_rows = quality.shape[1]
    block_cols = quality.shape[2]
    total_rows = block_rows * lax.axis_size("row")
    total_cols = block_cols * lax.axis_size("col")
    looked = jnp.zeros(quality.shape, jnp.float32)
    for label in range(class_score.shape[0]):
        looked = jnp.where(scene_class == label, class_score[label], looked)
    scores = looked + quality
    shift = jnp.max(scores, axis=0).astype(jnp.bfloat16).astype(jnp.float32)
    weights = jnp.exp(scores - shift[None])
    part_sums = jnp.sum(weights[:, None] * reflectance, axis=0)
    part_total = jnp.sum(weights, axis=0)
    packed = jnp.concatenate([part_sums, part_total[None], shift[None]], axis=0).astype(jnp.bfloat16)
    gathered = lax.all_gather(packed, "tm", axis=0).astype(jnp.float32)
    shifts = gathered[:, -1]
    scale = jnp.exp(shifts - jnp.max(shifts, axis=0)[None])
    band_sums = jnp.sum(scale[:, None] * gathered[:, :-2], axis=0)
    total_weight = jnp.sum(scale * gathered[:, -2], axis=0)
    composite = (band_sums / total_weight[None]).astype(jnp.bfloat16)

    row0 = lax.axis_index("row") * block_rows
    col0 = lax.axis_index("col") * block_cols
    widened = with_halo(composite, (("row", 1), ("col", 2)), HALO)
    first_map = masked_layer(widened, encode_first, row0 - HALO + 1, col0 - HALO + 1, total_rows, total_cols)
    skip_wide = masked_layer(first_map, encode_second, row0 - HALO + 2, col0 - HALO + 2, total_rows, total_cols)
    channels, wide_rows, wide_cols = skip_wide.shape
    pooled = jnp.mean(
        skip_wide.astype(jnp.float32).reshape(channels, wide_rows // 2, 2, wide_cols // 2, 2), axis=(2, 4)
    ).astype(jnp.bfloat16)
    coarse_halo = (HALO - 2) // 2
    crow0 = row0 // 2 - coarse_halo
    ccol0 = col0 // 2 - coarse_halo
    mid = masked_layer(pooled, middle_first, crow0 + 1, ccol0 + 1, total_rows // 2, total_cols // 2)
    deeper = masked_layer(mid, middle_second, crow0 + 2, ccol0 + 2, total_rows // 2, total_cols // 2)
    upsampled = jnp.repeat(jnp.repeat(deeper, 2, axis=1), 2, axis=2)
    up_halo = 2 * (coarse_halo - 2)
    upsampled = upsampled[:, up_halo - 1 : up_halo + block_rows + 1, up_halo - 1 : up_halo + block_cols + 1]
    skip_halo = HALO - 2
    skip = skip_wide[:, skip_halo - 1 : skip_halo + block_rows + 1, skip_halo - 1 : skip_halo + block_cols + 1]
    joined = jnp.concatenate([skip, upsampled], axis=0)
    decoded = jnp.maximum(valid_conv(joined, decode_kernel), 0.0).astype(jnp.bfloat16)
    return jnp.einsum(
        "oc,chw->ohw", head_weight, decoded, preferred_element_type=jnp.float32
    ).astype(jnp.bfloat16)


def solution(mesh):
    placed = (
        P("tm", None, "row", "col"),
        P("tm", "row", "col"),
        P("tm", "row", "col"),
        P(),
        P(),
        P(),
        P(),
        P(),
        P(),
        P(),
    )
    return jax.shard_map(
        shards, mesh=mesh, in_specs=placed, out_specs=P(None, "row", "col"), check_vma=False
    )
```

```python
import jax
import jax.numpy as jnp
from jax import lax
from jax.sharding import PartitionSpec as P

HALO = 8


def with_halo(cells, sides, width):
    for axis, dim in sides:
        count = lax.axis_size(axis)
        ends = count - 1
        head = lax.slice_in_dim(cells, 0, width, axis=dim)
        tail = lax.slice_in_dim(cells, cells.shape[dim] - width, cells.shape[dim], axis=dim)
        cells = jnp.concatenate(
            [
                lax.ppermute(tail, axis, [(i, (i + 1) % count) for i in range(ends)]),
                cells,
                lax.ppermute(head, axis, [((i + 1) % count, i) for i in range(ends)]),
            ],
            axis=dim,
        )
    return cells


def valid_conv(padded, kernel):
    return lax.conv_general_dilated(
        padded[None],
        kernel,
        (1, 1),
        "VALID",
        dimension_numbers=("NHWC", "HWOI", "NHWC"),
        preferred_element_type=jnp.float32,
    )[0]


def inside_mask(row_start, col_start, height, width, total_rows, total_cols):
    rows = row_start + jnp.arange(height, dtype=jnp.int32)
    cols = col_start + jnp.arange(width, dtype=jnp.int32)
    row_in = (rows >= 0) & (rows < total_rows)
    col_in = (cols >= 0) & (cols < total_cols)
    return (row_in[:, None] & col_in[None, :])[:, :, None]


def masked_layer(field, kernel, row_start, col_start, total_rows, total_cols):
    out = valid_conv(field, kernel)
    mask = inside_mask(row_start, col_start, out.shape[0], out.shape[1], total_rows, total_cols)
    return jnp.where(mask, jnp.maximum(out, 0.0), 0.0).astype(jnp.bfloat16)


def shards(
    reflectance,
    scene_class,
    quality,
    class_score,
    encode_first,
    encode_second,
    middle_first,
    middle_second,
    decode_kernel,
    head_weight,
):
    block_rows = quality.shape[1]
    block_cols = quality.shape[2]
    total_rows = block_rows * lax.axis_size("row")
    total_cols = block_cols * lax.axis_size("col")
    looked = jnp.zeros(quality.shape, jnp.float32)
    for label in range(class_score.shape[0]):
        looked = jnp.where(scene_class == label, class_score[label], looked)
    scores = looked + quality
    shift = jnp.max(scores, axis=0).astype(jnp.bfloat16).astype(jnp.float32)
    weights = jnp.exp(scores - shift[None])
    part_sums = jnp.sum(weights[:, None] * reflectance, axis=0)
    part_total = jnp.sum(weights, axis=0)
    packed = jnp.concatenate([part_sums, part_total[None], shift[None]], axis=0).astype(jnp.bfloat16)
    gathered = lax.all_gather(packed, "tm", axis=0).astype(jnp.float32)
    shifts = gathered[:, -1]
    scale = jnp.exp(shifts - jnp.max(shifts, axis=0)[None])
    band_sums = jnp.sum(scale[:, None] * gathered[:, :-2], axis=0)
    total_weight = jnp.sum(scale * gathered[:, -2], axis=0)
    composite = (band_sums / total_weight[None]).astype(jnp.bfloat16)

    row0 = lax.axis_index("row") * block_rows
    col0 = lax.axis_index("col") * block_cols
    widened = with_halo(composite.transpose(1, 2, 0), (("row", 0), ("col", 1)), HALO)
    first_map = masked_layer(widened, encode_first, row0 - HALO + 1, col0 - HALO + 1, total_rows, total_cols)
    skip_wide = masked_layer(first_map, encode_second, row0 - HALO + 2, col0 - HALO + 2, total_rows, total_cols)
    wide_rows, wide_cols, channels = skip_wide.shape
    pooled = jnp.mean(
        skip_wide.astype(jnp.float32).reshape(wide_rows // 2, 2, wide_cols // 2, 2, channels), axis=(1, 3)
    ).astype(jnp.bfloat16)
    coarse_halo = (HALO - 2) // 2
    crow0 = row0 // 2 - coarse_halo
    ccol0 = col0 // 2 - coarse_halo
    mid = masked_layer(pooled, middle_first, crow0 + 1, ccol0 + 1, total_rows // 2, total_cols // 2)
    deeper = masked_layer(mid, middle_second, crow0 + 2, ccol0 + 2, total_rows // 2, total_cols // 2)
    upsampled = jnp.repeat(jnp.repeat(deeper, 2, axis=0), 2, axis=1)
    up_halo = 2 * (coarse_halo - 2)
    upsampled = upsampled[up_halo - 1 : up_halo + block_rows + 1, up_halo - 1 : up_halo + block_cols + 1]
    skip_halo = HALO - 2
    skip = skip_wide[skip_halo - 1 : skip_halo + block_rows + 1, skip_halo - 1 : skip_halo + block_cols + 1]
    joined = jnp.concatenate([skip, upsampled], axis=2)
    decoded = jnp.maximum(valid_conv(joined, decode_kernel), 0.0).astype(jnp.bfloat16)
    return jnp.einsum(
        "oc,hwc->ohw", head_weight, decoded, preferred_element_type=jnp.float32
    ).astype(jnp.bfloat16)


def solution(mesh):
    placed = (
        P("tm", None, "row", "col"),
        P("tm", "row", "col"),
        P("tm", "row", "col"),
        P(),
        P(),
        P(),
        P(),
        P(),
        P(),
        P(),
    )
    return jax.shard_map(
        shards, mesh=mesh, in_specs=placed, out_specs=P(None, "row", "col"), check_vma=False
    )
```

```python
import jax
import jax.numpy as jnp
from jax import lax
from jax.sharding import PartitionSpec as P

HALO = 8


def with_halo(cells, sides, width):
    for axis, dim in sides:
        count = lax.axis_size(axis)
        ends = count - 1
        head = lax.slice_in_dim(cells, 0, width, axis=dim)
        tail = lax.slice_in_dim(cells, cells.shape[dim] - width, cells.shape[dim], axis=dim)
        cells = jnp.concatenate(
            [
                lax.ppermute(tail, axis, [(i, (i + 1) % count) for i in range(ends)]),
                cells,
                lax.ppermute(head, axis, [((i + 1) % count, i) for i in range(ends)]),
            ],
            axis=dim,
        )
    return cells


def valid_conv(padded, kernel):
    taps, _, outs, ins = kernel.shape[0], kernel.shape[1], kernel.shape[2], kernel.shape[3]
    height = padded.shape[1] - taps + 1
    width = padded.shape[2] - taps + 1
    patches = jnp.concatenate(
        [padded[:, a : a + height, e : e + width] for a in range(taps) for e in range(taps)], axis=0
    )
    flat = kernel.transpose(2, 0, 1, 3).reshape(outs, taps * taps * ins)
    return jnp.einsum("ok,khw->ohw", flat, patches, preferred_element_type=jnp.float32)


def pair_matrix(count, spread):
    wide = jnp.arange(count * 2, dtype=jnp.int32) // 2
    narrow = jnp.arange(count, dtype=jnp.int32)
    ones = (narrow[:, None] == wide[None, :]).astype(jnp.bfloat16)
    return ones if spread else ones.T


def inside_mask(row_start, col_start, height, width, total_rows, total_cols):
    rows = row_start + jnp.arange(height, dtype=jnp.int32)
    cols = col_start + jnp.arange(width, dtype=jnp.int32)
    row_in = (rows >= 0) & (rows < total_rows)
    col_in = (cols >= 0) & (cols < total_cols)
    return (row_in[:, None] & col_in[None, :])[None]


def masked_layer(field, kernel, row_start, col_start, total_rows, total_cols):
    out = valid_conv(field, kernel)
    mask = inside_mask(row_start, col_start, out.shape[1], out.shape[2], total_rows, total_cols)
    return jnp.where(mask, jnp.maximum(out, 0.0), 0.0).astype(jnp.bfloat16)


def shards(
    reflectance,
    scene_class,
    quality,
    class_score,
    encode_first,
    encode_second,
    middle_first,
    middle_second,
    decode_kernel,
    head_weight,
):
    block_rows = quality.shape[1]
    block_cols = quality.shape[2]
    total_rows = block_rows * lax.axis_size("row")
    total_cols = block_cols * lax.axis_size("col")
    looked = jnp.zeros(quality.shape, jnp.float32)
    for label in range(class_score.shape[0]):
        looked = jnp.where(scene_class == label, class_score[label], looked)
    scores = looked + quality
    shift = jnp.max(scores, axis=0).astype(jnp.bfloat16).astype(jnp.float32)
    weights = jnp.exp(scores - shift[None])
    part_sums = jnp.sum(weights[:, None] * reflectance, axis=0)
    part_total = jnp.sum(weights, axis=0)
    packed = jnp.concatenate([part_sums, part_total[None], shift[None]], axis=0).astype(jnp.bfloat16)
    gathered = lax.all_gather(packed, "tm", axis=0).astype(jnp.float32)
    shifts = gathered[:, -1]
    scale = jnp.exp(shifts - jnp.max(shifts, axis=0)[None])
    band_sums = jnp.sum(scale[:, None] * gathered[:, :-2], axis=0)
    total_weight = jnp.sum(scale * gathered[:, -2], axis=0)
    composite = (band_sums / total_weight[None]).astype(jnp.bfloat16)

    row0 = lax.axis_index("row") * block_rows
    col0 = lax.axis_index("col") * block_cols
    widened = with_halo(composite, (("row", 1), ("col", 2)), HALO)
    first_map = masked_layer(widened, encode_first, row0 - HALO + 1, col0 - HALO + 1, total_rows, total_cols)
    skip_wide = masked_layer(first_map, encode_second, row0 - HALO + 2, col0 - HALO + 2, total_rows, total_cols)
    channels, wide_rows, wide_cols = skip_wide.shape
    col_pairs = jnp.einsum(
        "chw,wv->chv", skip_wide, pair_matrix(wide_cols // 2, False), preferred_element_type=jnp.float32
    )
    pooled = (
        jnp.sum(col_pairs.reshape(channels, wide_rows // 2, 2, wide_cols // 2), axis=2) * 0.25
    ).astype(jnp.bfloat16)
    coarse_halo = (HALO - 2) // 2
    crow0 = row0 // 2 - coarse_halo
    ccol0 = col0 // 2 - coarse_halo
    mid = masked_layer(pooled, middle_first, crow0 + 1, ccol0 + 1, total_rows // 2, total_cols // 2)
    deeper = masked_layer(mid, middle_second, crow0 + 2, ccol0 + 2, total_rows // 2, total_cols // 2)
    deep_ch, deep_rows, deep_cols = deeper.shape
    spread = jnp.einsum(
        "chv,vw->chw", deeper, pair_matrix(deep_cols, True), preferred_element_type=jnp.float32
    ).astype(jnp.bfloat16)
    upsampled = jnp.broadcast_to(spread[:, :, None], (deep_ch, deep_rows, 2, 2 * deep_cols)).reshape(
        deep_ch, 2 * deep_rows, 2 * deep_cols
    )
    up_halo = 2 * (coarse_halo - 2)
    upsampled = upsampled[:, up_halo - 1 : up_halo + block_rows + 1, up_halo - 1 : up_halo + block_cols + 1]
    skip_halo = HALO - 2
    skip = skip_wide[:, skip_halo - 1 : skip_halo + block_rows + 1, skip_halo - 1 : skip_halo + block_cols + 1]
    joined = jnp.concatenate([skip, upsampled], axis=0)
    decoded = jnp.maximum(valid_conv(joined, decode_kernel), 0.0).astype(jnp.bfloat16)
    return jnp.einsum(
        "oc,chw->ohw", head_weight, decoded, preferred_element_type=jnp.float32
    ).astype(jnp.bfloat16)


def solution(mesh):
    placed = (
        P("tm", None, "row", "col"),
        P("tm", "row", "col"),
        P("tm", "row", "col"),
        P(),
        P(),
        P(),
        P(),
        P(),
        P(),
        P(),
    )
    return jax.shard_map(
        shards, mesh=mesh, in_specs=placed, out_specs=P(None, "row", "col"), check_vma=False
    )
```

```python
import jax
import jax.numpy as jnp
from jax import lax
from jax.sharding import PartitionSpec as P

HALO = 8


def with_halo(cells, sides, width):
    for axis, dim in sides:
        count = lax.axis_size(axis)
        ends = count - 1
        head = lax.slice_in_dim(cells, 0, width, axis=dim)
        tail = lax.slice_in_dim(cells, cells.shape[dim] - width, cells.shape[dim], axis=dim)
        cells = jnp.concatenate(
            [
                lax.ppermute(tail, axis, [(i, (i + 1) % count) for i in range(ends)]),
                cells,
                lax.ppermute(head, axis, [((i + 1) % count, i) for i in range(ends)]),
            ],
            axis=dim,
        )
    return cells


def valid_conv(padded, kernel):
    taps = kernel.shape[0]
    height = padded.shape[0] - taps + 1
    width = padded.shape[1] - taps + 1
    total = None
    for a in range(taps):
        for e in range(taps):
            term = jnp.einsum(
                "hwc,oc->hwo",
                padded[a : a + height, e : e + width],
                kernel[a, e],
                preferred_element_type=jnp.float32,
            )
            total = term if total is None else total + term
    return total


def inside_mask(row_start, col_start, height, width, total_rows, total_cols):
    rows = row_start + jnp.arange(height, dtype=jnp.int32)
    cols = col_start + jnp.arange(width, dtype=jnp.int32)
    row_in = (rows >= 0) & (rows < total_rows)
    col_in = (cols >= 0) & (cols < total_cols)
    return (row_in[:, None] & col_in[None, :])[:, :, None]


def masked_layer(field, kernel, row_start, col_start, total_rows, total_cols):
    out = valid_conv(field, kernel)
    mask = inside_mask(row_start, col_start, out.shape[0], out.shape[1], total_rows, total_cols)
    return jnp.where(mask, jnp.maximum(out, 0.0), 0.0).astype(jnp.bfloat16)


def shards(
    reflectance,
    scene_class,
    quality,
    class_score,
    encode_first,
    encode_second,
    middle_first,
    middle_second,
    decode_kernel,
    head_weight,
):
    block_rows = quality.shape[1]
    block_cols = quality.shape[2]
    total_rows = block_rows * lax.axis_size("row")
    total_cols = block_cols * lax.axis_size("col")
    looked = jnp.zeros(quality.shape, jnp.float32)
    for label in range(class_score.shape[0]):
        looked = jnp.where(scene_class == label, class_score[label], looked)
    scores = looked + quality
    shift = jnp.max(scores, axis=0).astype(jnp.bfloat16).astype(jnp.float32)
    weights = jnp.exp(scores - shift[None])
    part_sums = jnp.sum(weights[:, None] * reflectance, axis=0)
    part_total = jnp.sum(weights, axis=0)
    packed = jnp.concatenate([part_sums, part_total[None], shift[None]], axis=0).astype(jnp.bfloat16)
    gathered = lax.all_gather(packed, "tm", axis=0).astype(jnp.float32)
    shifts = gathered[:, -1]
    scale = jnp.exp(shifts - jnp.max(shifts, axis=0)[None])
    band_sums = jnp.sum(scale[:, None] * gathered[:, :-2], axis=0)
    total_weight = jnp.sum(scale * gathered[:, -2], axis=0)
    composite = (band_sums / total_weight[None]).astype(jnp.bfloat16)

    row0 = lax.axis_index("row") * block_rows
    col0 = lax.axis_index("col") * block_cols
    widened = with_halo(composite.transpose(1, 2, 0), (("row", 0), ("col", 1)), HALO)
    first_map = masked_layer(widened, encode_first, row0 - HALO + 1, col0 - HALO + 1, total_rows, total_cols)
    skip_wide = masked_layer(first_map, encode_second, row0 - HALO + 2, col0 - HALO + 2, total_rows, total_cols)
    wide_rows, wide_cols, channels = skip_wide.shape
    pooled = jnp.mean(
        skip_wide.astype(jnp.float32).reshape(wide_rows // 2, 2, wide_cols // 2, 2, channels), axis=(1, 3)
    ).astype(jnp.bfloat16)
    coarse_halo = (HALO - 2) // 2
    crow0 = row0 // 2 - coarse_halo
    ccol0 = col0 // 2 - coarse_halo
    mid = masked_layer(pooled, middle_first, crow0 + 1, ccol0 + 1, total_rows // 2, total_cols // 2)
    deeper = masked_layer(mid, middle_second, crow0 + 2, ccol0 + 2, total_rows // 2, total_cols // 2)
    upsampled = jnp.repeat(jnp.repeat(deeper, 2, axis=0), 2, axis=1)
    up_halo = 2 * (coarse_halo - 2)
    upsampled = upsampled[up_halo - 1 : up_halo + block_rows + 1, up_halo - 1 : up_halo + block_cols + 1]
    skip_halo = HALO - 2
    skip = skip_wide[skip_halo - 1 : skip_halo + block_rows + 1, skip_halo - 1 : skip_halo + block_cols + 1]
    joined = jnp.concatenate([skip, upsampled], axis=2)
    decoded = jnp.maximum(valid_conv(joined, decode_kernel), 0.0).astype(jnp.bfloat16)
    return jnp.einsum(
        "oc,hwc->ohw", head_weight, decoded, preferred_element_type=jnp.float32
    ).astype(jnp.bfloat16)


def solution(mesh):
    placed = (
        P("tm", None, "row", "col"),
        P("tm", "row", "col"),
        P("tm", "row", "col"),
        P(),
        P(),
        P(),
        P(),
        P(),
        P(),
        P(),
    )
    return jax.shard_map(
        shards, mesh=mesh, in_specs=placed, out_specs=P(None, "row", "col"), check_vma=False
    )
```

```python
import jax
import jax.numpy as jnp
from jax import lax
from jax.sharding import PartitionSpec as P

HALO = 8


def with_halo(cells, sides, width):
    for axis, dim in sides:
        count = lax.axis_size(axis)
        ends = count - 1
        head = lax.slice_in_dim(cells, 0, width, axis=dim)
        tail = lax.slice_in_dim(cells, cells.shape[dim] - width, cells.shape[dim], axis=dim)
        cells = jnp.concatenate(
            [
                lax.ppermute(tail, axis, [(i, (i + 1) % count) for i in range(ends)]),
                cells,
                lax.ppermute(head, axis, [((i + 1) % count, i) for i in range(ends)]),
            ],
            axis=dim,
        )
    return cells


def valid_conv(padded, kernel):
    taps = kernel.shape[0]
    height = padded.shape[0] - taps + 1
    width = padded.shape[1] - taps + 1
    total = None
    for a in range(taps):
        for e in range(taps):
            term = jnp.einsum(
                "hwc,oc->hwo",
                padded[a : a + height, e : e + width],
                kernel[a, e],
                preferred_element_type=jnp.float32,
            )
            total = term if total is None else total + term
    return total


def pair_matrix(narrow, wide, offset):
    pick = (jnp.arange(wide, dtype=jnp.int32) + offset) // 2
    return (jnp.arange(narrow, dtype=jnp.int32)[:, None] == pick[None, :]).astype(jnp.bfloat16)


def inside_mask(row_start, col_start, height, width, total_rows, total_cols):
    rows = row_start + jnp.arange(height, dtype=jnp.int32)
    cols = col_start + jnp.arange(width, dtype=jnp.int32)
    row_in = (rows >= 0) & (rows < total_rows)
    col_in = (cols >= 0) & (cols < total_cols)
    return (row_in[:, None] & col_in[None, :])[:, :, None]


def masked_layer(field, kernel, row_start, col_start, total_rows, total_cols):
    out = valid_conv(field, kernel)
    mask = inside_mask(row_start, col_start, out.shape[0], out.shape[1], total_rows, total_cols)
    return jnp.where(mask, jnp.maximum(out, 0.0), 0.0).astype(jnp.bfloat16)


def shards(
    reflectance,
    scene_class,
    quality,
    class_score,
    encode_first,
    encode_second,
    middle_first,
    middle_second,
    decode_kernel,
    head_weight,
):
    block_rows = quality.shape[1]
    block_cols = quality.shape[2]
    total_rows = block_rows * lax.axis_size("row")
    total_cols = block_cols * lax.axis_size("col")
    looked = jnp.zeros(quality.shape, jnp.float32)
    for label in range(class_score.shape[0]):
        looked = jnp.where(scene_class == label, class_score[label], looked)
    scores = looked + quality
    shift = jnp.max(scores, axis=0).astype(jnp.bfloat16).astype(jnp.float32)
    weights = jnp.exp(scores - shift[None])
    part_sums = jnp.sum(weights[:, None] * reflectance, axis=0)
    part_total = jnp.sum(weights, axis=0)
    packed = jnp.concatenate([part_sums, part_total[None], shift[None]], axis=0).astype(jnp.bfloat16)
    gathered = lax.all_gather(packed, "tm", axis=0).astype(jnp.float32)
    shifts = gathered[:, -1]
    scale = jnp.exp(shifts - jnp.max(shifts, axis=0)[None])
    band_sums = jnp.sum(scale[:, None] * gathered[:, :-2], axis=0)
    total_weight = jnp.sum(scale * gathered[:, -2], axis=0)
    composite = (band_sums / total_weight[None]).astype(jnp.bfloat16)

    row0 = lax.axis_index("row") * block_rows
    col0 = lax.axis_index("col") * block_cols
    widened = with_halo(composite.transpose(1, 2, 0), (("row", 0), ("col", 1)), HALO)
    first_map = masked_layer(widened, encode_first, row0 - HALO + 1, col0 - HALO + 1, total_rows, total_cols)
    skip_wide = masked_layer(first_map, encode_second, row0 - HALO + 2, col0 - HALO + 2, total_rows, total_cols)
    wide_rows, wide_cols, channels = skip_wide.shape
    col_pairs = jnp.einsum(
        "vw,hwc->hvc", pair_matrix(wide_cols // 2, wide_cols, 0), skip_wide, preferred_element_type=jnp.float32
    )
    pooled = (
        jnp.sum(col_pairs.reshape(wide_rows // 2, 2, wide_cols // 2, channels), axis=1) * 0.25
    ).astype(jnp.bfloat16)
    coarse_halo = (HALO - 2) // 2
    crow0 = row0 // 2 - coarse_halo
    ccol0 = col0 // 2 - coarse_halo
    mid = masked_layer(pooled, middle_first, crow0 + 1, ccol0 + 1, total_rows // 2, total_cols // 2)
    deeper = masked_layer(mid, middle_second, crow0 + 2, ccol0 + 2, total_rows // 2, total_cols // 2)
    up_halo = 2 * (coarse_halo - 2)
    deep_rows, deep_cols, deep_ch = deeper.shape
    spread = jnp.einsum(
        "wv,hvc->hwc",
        pair_matrix(deep_cols, block_cols + 2, up_halo - 1).T,
        deeper,
        preferred_element_type=jnp.float32,
    ).astype(jnp.bfloat16)
    upsampled = jnp.broadcast_to(spread[:, None], (deep_rows, 2, block_cols + 2, deep_ch)).reshape(
        2 * deep_rows, block_cols + 2, deep_ch
    )[up_halo - 1 : up_halo + block_rows + 1]
    skip_halo = HALO - 2
    skip = skip_wide[skip_halo - 1 : skip_halo + block_rows + 1, skip_halo - 1 : skip_halo + block_cols + 1]
    joined = jnp.concatenate([skip, upsampled], axis=2)
    decoded = jnp.maximum(valid_conv(joined, decode_kernel), 0.0).astype(jnp.bfloat16)
    return jnp.einsum(
        "oc,hwc->ohw", head_weight, decoded, preferred_element_type=jnp.float32
    ).astype(jnp.bfloat16)


def solution(mesh):
    placed = (
        P("tm", None, "row", "col"),
        P("tm", "row", "col"),
        P("tm", "row", "col"),
        P(),
        P(),
        P(),
        P(),
        P(),
        P(),
        P(),
    )
    return jax.shard_map(
        shards, mesh=mesh, in_specs=placed, out_specs=P(None, "row", "col"), check_vma=False
    )
```

```python
import jax
import jax.numpy as jnp
from jax import lax
from jax.experimental import pallas as pl
from jax.experimental.pallas import tpu as pltpu
from jax.sharding import PartitionSpec as P

HALO = 8


def with_halo(cells, sides, width):
    for axis, dim in sides:
        count = lax.axis_size(axis)
        ends = count - 1
        head = lax.slice_in_dim(cells, 0, width, axis=dim)
        tail = lax.slice_in_dim(cells, cells.shape[dim] - width, cells.shape[dim], axis=dim)
        cells = jnp.concatenate(
            [
                lax.ppermute(tail, axis, [(i, (i + 1) % count) for i in range(ends)]),
                cells,
                lax.ppermute(head, axis, [((i + 1) % count, i) for i in range(ends)]),
            ],
            axis=dim,
        )
    return cells


def valid_conv(padded, kernel):
    taps = kernel.shape[0]
    height = padded.shape[0] - taps + 1
    width = padded.shape[1] - taps + 1
    total = None
    for a in range(taps):
        for e in range(taps):
            term = jnp.einsum(
                "hwc,oc->hwo",
                padded[a : a + height, e : e + width],
                kernel[a, e],
                preferred_element_type=jnp.float32,
            )
            total = term if total is None else total + term
    return total


def pair_matrix(narrow, wide, offset):
    pick = (jnp.arange(wide, dtype=jnp.int32) + offset) // 2
    return (jnp.arange(narrow, dtype=jnp.int32)[:, None] == pick[None, :]).astype(jnp.bfloat16)


def composite_kernel(score_ref, bands_ref, class_ref, quality_ref, out_ref):
    dates, bands, rows, _ = bands_ref.shape
    classes = score_ref.shape[0]
    step = 16

    def chunk(index, carry):
        at = pl.ds(pl.multiple_of(index * step, step), step)
        scores = []
        for date in range(dates):
            label = class_ref[date, at, :]
            looked = jnp.zeros(label.shape, jnp.float32)
            for k in range(classes):
                looked = jnp.where(label == k, score_ref[k], looked)
            scores.append(looked + quality_ref[date, at, :])
        top = scores[0]
        for score in scores[1:]:
            top = jnp.maximum(top, score)
        shift = top.astype(jnp.bfloat16).astype(jnp.float32)
        weights = [jnp.exp(score - shift) for score in scores]
        total = weights[0]
        for weight in weights[1:]:
            total = total + weight
        def one_band(band, inner):
            acc = weights[0] * bands_ref[0, band, at, :].astype(jnp.float32)
            for date in range(1, dates):
                acc = acc + weights[date] * bands_ref[date, band, at, :].astype(jnp.float32)
            out_ref[band, at, :] = acc.astype(jnp.bfloat16)
            return inner

        lax.fori_loop(0, bands, one_band, 0)
        out_ref[bands, at, :] = total.astype(jnp.bfloat16)
        out_ref[bands + 1, at, :] = shift.astype(jnp.bfloat16)
        return carry

    lax.fori_loop(0, rows // step, chunk, 0)


def local_sums(class_score, reflectance, scene_class, quality):
    dates, bands, rows, cols = reflectance.shape
    vmem = pl.BlockSpec(memory_space=pltpu.VMEM)
    return pl.pallas_call(
        composite_kernel,
        out_shape=jax.ShapeDtypeStruct((bands + 2, rows, cols), jnp.bfloat16),
        in_specs=[pl.BlockSpec(memory_space=pltpu.SMEM), vmem, vmem, vmem],
        out_specs=vmem,
    )(class_score, reflectance, scene_class, quality)


def inside_mask(row_start, col_start, height, width, total_rows, total_cols):
    rows = row_start + jnp.arange(height, dtype=jnp.int32)
    cols = col_start + jnp.arange(width, dtype=jnp.int32)
    row_in = (rows >= 0) & (rows < total_rows)
    col_in = (cols >= 0) & (cols < total_cols)
    return (row_in[:, None] & col_in[None, :])[:, :, None]


def masked_layer(field, kernel, row_start, col_start, total_rows, total_cols):
    out = valid_conv(field, kernel)
    mask = inside_mask(row_start, col_start, out.shape[0], out.shape[1], total_rows, total_cols)
    return jnp.where(mask, jnp.maximum(out, 0.0), 0.0).astype(jnp.bfloat16)


def shards(
    reflectance,
    scene_class,
    quality,
    class_score,
    encode_first,
    encode_second,
    middle_first,
    middle_second,
    decode_kernel,
    head_weight,
):
    block_rows = quality.shape[1]
    block_cols = quality.shape[2]
    total_rows = block_rows * lax.axis_size("row")
    total_cols = block_cols * lax.axis_size("col")
    packed = local_sums(class_score, reflectance, scene_class, quality)
    gathered = lax.all_gather(packed, "tm", axis=0).astype(jnp.float32)
    shifts = gathered[:, -1]
    scale = jnp.exp(shifts - jnp.max(shifts, axis=0)[None])
    band_sums = jnp.sum(scale[:, None] * gathered[:, :-2], axis=0)
    total_weight = jnp.sum(scale * gathered[:, -2], axis=0)
    composite = (band_sums / total_weight[None]).astype(jnp.bfloat16)

    row0 = lax.axis_index("row") * block_rows
    col0 = lax.axis_index("col") * block_cols
    widened = with_halo(composite.transpose(1, 2, 0), (("row", 0), ("col", 1)), HALO)
    first_map = masked_layer(widened, encode_first, row0 - HALO + 1, col0 - HALO + 1, total_rows, total_cols)
    skip_wide = masked_layer(first_map, encode_second, row0 - HALO + 2, col0 - HALO + 2, total_rows, total_cols)
    wide_rows, wide_cols, channels = skip_wide.shape
    col_pairs = jnp.einsum(
        "vw,hwc->hvc", pair_matrix(wide_cols // 2, wide_cols, 0), skip_wide, preferred_element_type=jnp.float32
    )
    pooled = (
        jnp.sum(col_pairs.reshape(wide_rows // 2, 2, wide_cols // 2, channels), axis=1) * 0.25
    ).astype(jnp.bfloat16)
    coarse_halo = (HALO - 2) // 2
    crow0 = row0 // 2 - coarse_halo
    ccol0 = col0 // 2 - coarse_halo
    mid = masked_layer(pooled, middle_first, crow0 + 1, ccol0 + 1, total_rows // 2, total_cols // 2)
    deeper = masked_layer(mid, middle_second, crow0 + 2, ccol0 + 2, total_rows // 2, total_cols // 2)
    up_halo = 2 * (coarse_halo - 2)
    deep_rows, deep_cols, deep_ch = deeper.shape
    spread = jnp.einsum(
        "wv,hvc->hwc",
        pair_matrix(deep_cols, block_cols + 2, up_halo - 1).T,
        deeper,
        preferred_element_type=jnp.float32,
    ).astype(jnp.bfloat16)
    upsampled = jnp.broadcast_to(spread[:, None], (deep_rows, 2, block_cols + 2, deep_ch)).reshape(
        2 * deep_rows, block_cols + 2, deep_ch
    )[up_halo - 1 : up_halo + block_rows + 1]
    skip_halo = HALO - 2
    skip = skip_wide[skip_halo - 1 : skip_halo + block_rows + 1, skip_halo - 1 : skip_halo + block_cols + 1]
    joined = jnp.concatenate([skip, upsampled], axis=2)
    decoded = jnp.maximum(valid_conv(joined, decode_kernel), 0.0).astype(jnp.bfloat16)
    return jnp.einsum(
        "oc,hwc->ohw", head_weight, decoded, preferred_element_type=jnp.float32
    ).astype(jnp.bfloat16)


def solution(mesh):
    placed = (
        P("tm", None, "row", "col"),
        P("tm", "row", "col"),
        P("tm", "row", "col"),
        P(),
        P(),
        P(),
        P(),
        P(),
        P(),
        P(),
    )
    return jax.shard_map(
        shards, mesh=mesh, in_specs=placed, out_specs=P(None, "row", "col"), check_vma=False
    )
```

```python
import jax
import jax.numpy as jnp
from jax import lax
from jax.experimental import pallas as pl
from jax.experimental.pallas import tpu as pltpu
from jax.sharding import PartitionSpec as P

HALO = 8


def with_halo(cells, sides, width):
    for axis, dim in sides:
        count = lax.axis_size(axis)
        ends = count - 1
        head = lax.slice_in_dim(cells, 0, width, axis=dim)
        tail = lax.slice_in_dim(cells, cells.shape[dim] - width, cells.shape[dim], axis=dim)
        cells = jnp.concatenate(
            [
                lax.ppermute(tail, axis, [(i, (i + 1) % count) for i in range(ends)]),
                cells,
                lax.ppermute(head, axis, [((i + 1) % count, i) for i in range(ends)]),
            ],
            axis=dim,
        )
    return cells


def valid_conv(padded, kernel, looped=False):
    taps = kernel.shape[0]
    height = padded.shape[0] - taps + 1
    width = padded.shape[1] - taps + 1

    def row_tap(a, total):
        rows = lax.dynamic_slice_in_dim(padded, a, height, axis=0)
        for e in range(taps):
            term = jnp.einsum(
                "hwc,oc->hwo",
                rows[:, e : e + width],
                kernel[a, e],
                preferred_element_type=jnp.float32,
            )
            total = term if total is None else total + term
        return total

    if not looped:
        total = None
        for a in range(taps):
            total = row_tap(a, total)
        return total
    start = jnp.zeros((height, width, kernel.shape[2]), jnp.float32)
    return lax.fori_loop(0, taps, row_tap, start)


def pair_matrix(narrow, wide, offset):
    pick = (jnp.arange(wide, dtype=jnp.int32) + offset) // 2
    return (jnp.arange(narrow, dtype=jnp.int32)[:, None] == pick[None, :]).astype(jnp.bfloat16)


def composite_kernel(score_ref, bands_ref, class_ref, quality_ref, out_ref, acc_ref):
    dates, bands, rows, _ = bands_ref.shape
    classes = score_ref.shape[0]
    step = acc_ref.shape[1]

    def chunk(index, carry):
        at = pl.ds(pl.multiple_of(index * step, step), step)

        def score(date):
            label = class_ref[date, at, :]
            looked = jnp.zeros(label.shape, jnp.float32)
            for k in range(classes):
                looked = jnp.where(label == k, score_ref[k], looked)
            return looked + quality_ref[date, at, :]

        top = lax.fori_loop(1, dates, lambda date, top: jnp.maximum(top, score(date)), score(0))
        shift = top.astype(jnp.bfloat16).astype(jnp.float32)
        acc_ref[...] = jnp.zeros(acc_ref.shape, jnp.float32)

        def one_date(date, total):
            weight = jnp.exp(score(date) - shift)
            for band in range(bands):
                acc_ref[band] += weight * bands_ref[date, band, at, :].astype(jnp.float32)
            return total + weight

        total = lax.fori_loop(0, dates, one_date, jnp.zeros(shift.shape, jnp.float32))
        out_ref[pl.ds(0, bands), at, :] = acc_ref[...].astype(jnp.bfloat16)
        out_ref[bands, at, :] = total.astype(jnp.bfloat16)
        out_ref[bands + 1, at, :] = shift.astype(jnp.bfloat16)
        return carry

    lax.fori_loop(0, rows // step, chunk, 0)


def local_sums(class_score, reflectance, scene_class, quality):
    dates, bands, rows, cols = reflectance.shape
    vmem = pl.BlockSpec(memory_space=pltpu.VMEM)
    return pl.pallas_call(
        composite_kernel,
        out_shape=jax.ShapeDtypeStruct((bands + 2, rows, cols), jnp.bfloat16),
        in_specs=[pl.BlockSpec(memory_space=pltpu.SMEM), vmem, vmem, vmem],
        out_specs=vmem,
        scratch_shapes=[pltpu.VMEM((bands, 16, cols), jnp.float32)],
    )(class_score, reflectance, scene_class, quality)


def inside_mask(row_start, col_start, height, width, total_rows, total_cols):
    rows = row_start + jnp.arange(height, dtype=jnp.int32)
    cols = col_start + jnp.arange(width, dtype=jnp.int32)
    row_in = (rows >= 0) & (rows < total_rows)
    col_in = (cols >= 0) & (cols < total_cols)
    return (row_in[:, None] & col_in[None, :])[:, :, None]


def masked_layer(field, kernel, row_start, col_start, total_rows, total_cols, looped=False):
    out = valid_conv(field, kernel, looped)
    mask = inside_mask(row_start, col_start, out.shape[0], out.shape[1], total_rows, total_cols)
    return jnp.where(mask, jnp.maximum(out, 0.0), 0.0).astype(jnp.bfloat16)


def shards(
    reflectance,
    scene_class,
    quality,
    class_score,
    encode_first,
    encode_second,
    middle_first,
    middle_second,
    decode_kernel,
    head_weight,
):
    block_rows = quality.shape[1]
    block_cols = quality.shape[2]
    total_rows = block_rows * lax.axis_size("row")
    total_cols = block_cols * lax.axis_size("col")
    packed = local_sums(class_score, reflectance, scene_class, quality)
    gathered = lax.all_gather(packed, "tm", axis=0).astype(jnp.float32)
    shifts = gathered[:, -1]
    scale = jnp.exp(shifts - jnp.max(shifts, axis=0)[None])
    band_sums = jnp.sum(scale[:, None] * gathered[:, :-2], axis=0)
    total_weight = jnp.sum(scale * gathered[:, -2], axis=0)
    composite = (band_sums / total_weight[None]).astype(jnp.bfloat16)

    row0 = lax.axis_index("row") * block_rows
    col0 = lax.axis_index("col") * block_cols
    widened = with_halo(composite.transpose(1, 2, 0), (("row", 0), ("col", 1)), HALO)
    first_map = masked_layer(widened, encode_first, row0 - HALO + 1, col0 - HALO + 1, total_rows, total_cols)
    skip_wide = masked_layer(first_map, encode_second, row0 - HALO + 2, col0 - HALO + 2, total_rows, total_cols)
    wide_rows, wide_cols, channels = skip_wide.shape
    col_pairs = jnp.einsum(
        "vw,hwc->hvc", pair_matrix(wide_cols // 2, wide_cols, 0), skip_wide, preferred_element_type=jnp.float32
    )
    pooled = (
        jnp.sum(col_pairs.reshape(wide_rows // 2, 2, wide_cols // 2, channels), axis=1) * 0.25
    ).astype(jnp.bfloat16)
    coarse_halo = (HALO - 2) // 2
    crow0 = row0 // 2 - coarse_halo
    ccol0 = col0 // 2 - coarse_halo
    mid = masked_layer(pooled, middle_first, crow0 + 1, ccol0 + 1, total_rows // 2, total_cols // 2, True)
    deeper = masked_layer(mid, middle_second, crow0 + 2, ccol0 + 2, total_rows // 2, total_cols // 2, True)
    up_halo = 2 * (coarse_halo - 2)
    deep_rows, deep_cols, deep_ch = deeper.shape
    spread = jnp.einsum(
        "wv,hvc->hwc",
        pair_matrix(deep_cols, block_cols + 2, up_halo - 1).T,
        deeper,
        preferred_element_type=jnp.float32,
    ).astype(jnp.bfloat16)
    upsampled = jnp.broadcast_to(spread[:, None], (deep_rows, 2, block_cols + 2, deep_ch)).reshape(
        2 * deep_rows, block_cols + 2, deep_ch
    )[up_halo - 1 : up_halo + block_rows + 1]
    skip_halo = HALO - 2
    skip = skip_wide[skip_halo - 1 : skip_halo + block_rows + 1, skip_halo - 1 : skip_halo + block_cols + 1]
    joined = jnp.concatenate([skip, upsampled], axis=2)
    decoded = jnp.maximum(valid_conv(joined, decode_kernel), 0.0).astype(jnp.bfloat16)
    return jnp.einsum(
        "oc,hwc->ohw", head_weight, decoded, preferred_element_type=jnp.float32
    ).astype(jnp.bfloat16)


def solution(mesh):
    placed = (
        P("tm", None, "row", "col"),
        P("tm", "row", "col"),
        P("tm", "row", "col"),
        P(),
        P(),
        P(),
        P(),
        P(),
        P(),
        P(),
    )
    return jax.shard_map(
        shards, mesh=mesh, in_specs=placed, out_specs=P(None, "row", "col"), check_vma=False
    )
```

```python
import jax
import jax.numpy as jnp
from jax import lax
from jax.experimental import pallas as pl
from jax.experimental.pallas import tpu as pltpu
from jax.sharding import PartitionSpec as P

HALO = 8


def with_halo(cells, sides, width):
    for axis, dim in sides:
        count = lax.axis_size(axis)
        ends = count - 1
        head = lax.slice_in_dim(cells, 0, width, axis=dim)
        tail = lax.slice_in_dim(cells, cells.shape[dim] - width, cells.shape[dim], axis=dim)
        cells = jnp.concatenate(
            [
                lax.ppermute(tail, axis, [(i, (i + 1) % count) for i in range(ends)]),
                cells,
                lax.ppermute(head, axis, [((i + 1) % count, i) for i in range(ends)]),
            ],
            axis=dim,
        )
    return cells


def valid_conv(padded, kernel):
    taps = kernel.shape[0]
    height = padded.shape[0] - taps + 1
    width = padded.shape[1] - taps + 1
    total = None
    for a in range(taps):
        for e in range(taps):
            term = jnp.einsum(
                "hwc,oc->hwo",
                padded[a : a + height, e : e + width],
                kernel[a, e],
                preferred_element_type=jnp.float32,
            )
            total = term if total is None else total + term
    return total


def pair_matrix(narrow, wide, offset):
    pick = (jnp.arange(wide, dtype=jnp.int32) + offset) // 2
    return (jnp.arange(narrow, dtype=jnp.int32)[:, None] == pick[None, :]).astype(jnp.bfloat16)


def weight_kernel(score_ref, class_ref, quality_ref, weight_ref, shift_ref):
    dates, rows, _ = class_ref.shape
    classes = score_ref.shape[0]
    step = 8

    def chunk(index, carry):
        at = pl.ds(pl.multiple_of(index * step, step), step)

        def score(date):
            label = class_ref[date, at, :]
            looked = jnp.zeros(label.shape, jnp.float32)
            for k in range(classes):
                looked = jnp.where(label == k, score_ref[k], looked)
            return looked + quality_ref[date, at, :]

        top = lax.fori_loop(1, dates, lambda date, top: jnp.maximum(top, score(date)), score(0))
        shift = top.astype(jnp.bfloat16).astype(jnp.float32)
        shift_ref[at, :] = shift

        def one_date(date, inner):
            weight_ref[date, at, :] = jnp.exp(score(date) - shift)
            return inner

        lax.fori_loop(0, dates, one_date, 0)
        return carry

    lax.fori_loop(0, rows // step, chunk, 0)


def shifted_weights(class_score, scene_class, quality):
    dates, rows, cols = quality.shape
    vmem = pl.BlockSpec(memory_space=pltpu.VMEM)
    return pl.pallas_call(
        weight_kernel,
        out_shape=(
            jax.ShapeDtypeStruct((dates, rows, cols), jnp.float32),
            jax.ShapeDtypeStruct((rows, cols), jnp.float32),
        ),
        in_specs=[pl.BlockSpec(memory_space=pltpu.SMEM), vmem, vmem],
        out_specs=(vmem, vmem),
    )(class_score, scene_class, quality)


def inside_mask(row_start, col_start, height, width, total_rows, total_cols):
    rows = row_start + jnp.arange(height, dtype=jnp.int32)
    cols = col_start + jnp.arange(width, dtype=jnp.int32)
    row_in = (rows >= 0) & (rows < total_rows)
    col_in = (cols >= 0) & (cols < total_cols)
    return (row_in[:, None] & col_in[None, :])[:, :, None]


def masked_layer(field, kernel, row_start, col_start, total_rows, total_cols):
    out = valid_conv(field, kernel)
    mask = inside_mask(row_start, col_start, out.shape[0], out.shape[1], total_rows, total_cols)
    return jnp.where(mask, jnp.maximum(out, 0.0), 0.0).astype(jnp.bfloat16)


def shards(
    reflectance,
    scene_class,
    quality,
    class_score,
    encode_first,
    encode_second,
    middle_first,
    middle_second,
    decode_kernel,
    head_weight,
):
    block_rows = quality.shape[1]
    block_cols = quality.shape[2]
    total_rows = block_rows * lax.axis_size("row")
    total_cols = block_cols * lax.axis_size("col")
    weights, shift = shifted_weights(class_score, scene_class, quality)
    part_sums = jnp.sum(weights[:, None] * reflectance, axis=0)
    part_total = jnp.sum(weights, axis=0)
    packed = jnp.concatenate([part_sums, part_total[None], shift[None]], axis=0).astype(jnp.bfloat16)
    gathered = lax.all_gather(packed, "tm", axis=0).astype(jnp.float32)
    shifts = gathered[:, -1]
    scale = jnp.exp(shifts - jnp.max(shifts, axis=0)[None])
    band_sums = jnp.sum(scale[:, None] * gathered[:, :-2], axis=0)
    total_weight = jnp.sum(scale * gathered[:, -2], axis=0)
    composite = (band_sums / total_weight[None]).astype(jnp.bfloat16)

    row0 = lax.axis_index("row") * block_rows
    col0 = lax.axis_index("col") * block_cols
    widened = with_halo(composite.transpose(1, 2, 0), (("row", 0), ("col", 1)), HALO)
    first_map = masked_layer(widened, encode_first, row0 - HALO + 1, col0 - HALO + 1, total_rows, total_cols)
    skip_wide = masked_layer(first_map, encode_second, row0 - HALO + 2, col0 - HALO + 2, total_rows, total_cols)
    wide_rows, wide_cols, channels = skip_wide.shape
    col_pairs = jnp.einsum(
        "vw,hwc->hvc", pair_matrix(wide_cols // 2, wide_cols, 0), skip_wide, preferred_element_type=jnp.float32
    )
    pooled = (
        jnp.sum(col_pairs.reshape(wide_rows // 2, 2, wide_cols // 2, channels), axis=1) * 0.25
    ).astype(jnp.bfloat16)
    coarse_halo = (HALO - 2) // 2
    crow0 = row0 // 2 - coarse_halo
    ccol0 = col0 // 2 - coarse_halo
    mid = masked_layer(pooled, middle_first, crow0 + 1, ccol0 + 1, total_rows // 2, total_cols // 2)
    deeper = masked_layer(mid, middle_second, crow0 + 2, ccol0 + 2, total_rows // 2, total_cols // 2)
    up_halo = 2 * (coarse_halo - 2)
    deep_rows, deep_cols, deep_ch = deeper.shape
    spread = jnp.einsum(
        "wv,hvc->hwc",
        pair_matrix(deep_cols, block_cols + 2, up_halo - 1).T,
        deeper,
        preferred_element_type=jnp.float32,
    ).astype(jnp.bfloat16)
    upsampled = jnp.broadcast_to(spread[:, None], (deep_rows, 2, block_cols + 2, deep_ch)).reshape(
        2 * deep_rows, block_cols + 2, deep_ch
    )[up_halo - 1 : up_halo + block_rows + 1]
    skip_halo = HALO - 2
    skip = skip_wide[skip_halo - 1 : skip_halo + block_rows + 1, skip_halo - 1 : skip_halo + block_cols + 1]
    joined = jnp.concatenate([skip, upsampled], axis=2)
    decoded = jnp.maximum(valid_conv(joined, decode_kernel), 0.0).astype(jnp.bfloat16)
    return jnp.einsum(
        "oc,hwc->ohw", head_weight, decoded, preferred_element_type=jnp.float32
    ).astype(jnp.bfloat16)


def solution(mesh):
    placed = (
        P("tm", None, "row", "col"),
        P("tm", "row", "col"),
        P("tm", "row", "col"),
        P(),
        P(),
        P(),
        P(),
        P(),
        P(),
        P(),
    )
    return jax.shard_map(
        shards, mesh=mesh, in_specs=placed, out_specs=P(None, "row", "col"), check_vma=False
    )
```

```python
import jax
import jax.numpy as jnp
from jax import lax
from jax.experimental import pallas as pl
from jax.experimental.pallas import tpu as pltpu
from jax.sharding import PartitionSpec as P

HALO = 8


def with_halo(cells, sides, width):
    for axis, dim in sides:
        count = lax.axis_size(axis)
        ends = count - 1
        head = lax.slice_in_dim(cells, 0, width, axis=dim)
        tail = lax.slice_in_dim(cells, cells.shape[dim] - width, cells.shape[dim], axis=dim)
        if count == 2:
            first = lax.axis_index(axis) == 0
            got = lax.ppermute(jnp.where(first, tail, head), axis, [(0, 1), (1, 0)])
            empty = jnp.zeros_like(got)
            cells = jnp.concatenate(
                [jnp.where(first, empty, got), cells, jnp.where(first, got, empty)], axis=dim
            )
            continue
        cells = jnp.concatenate(
            [
                lax.ppermute(tail, axis, [(i, (i + 1) % count) for i in range(ends)]),
                cells,
                lax.ppermute(head, axis, [((i + 1) % count, i) for i in range(ends)]),
            ],
            axis=dim,
        )
    return cells


def valid_conv(padded, kernel):
    taps = kernel.shape[0]
    height = padded.shape[0] - taps + 1
    width = padded.shape[1] - taps + 1
    total = None
    for a in range(taps):
        for e in range(taps):
            term = jnp.einsum(
                "hwc,oc->hwo",
                padded[a : a + height, e : e + width],
                kernel[a, e],
                preferred_element_type=jnp.float32,
            )
            total = term if total is None else total + term
    return total


def pair_matrix(narrow, wide, offset):
    pick = (jnp.arange(wide, dtype=jnp.int32) + offset) // 2
    return (jnp.arange(narrow, dtype=jnp.int32)[:, None] == pick[None, :]).astype(jnp.bfloat16)


def weight_kernel(score_ref, class_ref, quality_ref, weight_ref, shift_ref):
    dates, rows, _ = class_ref.shape
    classes = score_ref.shape[0]
    step = 8

    def chunk(index, carry):
        at = pl.ds(pl.multiple_of(index * step, step), step)

        def score(date):
            label = class_ref[date, at, :]
            looked = jnp.zeros(label.shape, jnp.float32)
            for k in range(classes):
                looked = jnp.where(label == k, score_ref[k], looked)
            return looked + quality_ref[date, at, :]

        top = lax.fori_loop(1, dates, lambda date, top: jnp.maximum(top, score(date)), score(0))
        shift = top.astype(jnp.bfloat16).astype(jnp.float32)
        shift_ref[at, :] = shift

        def one_date(date, inner):
            weight_ref[date, at, :] = jnp.exp(score(date) - shift)
            return inner

        lax.fori_loop(0, dates, one_date, 0)
        return carry

    lax.fori_loop(0, rows // step, chunk, 0)


def shifted_weights(class_score, scene_class, quality):
    dates, rows, cols = quality.shape
    vmem = pl.BlockSpec(memory_space=pltpu.VMEM)
    return pl.pallas_call(
        weight_kernel,
        out_shape=(
            jax.ShapeDtypeStruct((dates, rows, cols), jnp.float32),
            jax.ShapeDtypeStruct((rows, cols), jnp.float32),
        ),
        in_specs=[pl.BlockSpec(memory_space=pltpu.SMEM), vmem, vmem],
        out_specs=(vmem, vmem),
    )(class_score, scene_class, quality)


def inside_mask(row_start, col_start, height, width, total_rows, total_cols):
    rows = row_start + jnp.arange(height, dtype=jnp.int32)
    cols = col_start + jnp.arange(width, dtype=jnp.int32)
    row_in = (rows >= 0) & (rows < total_rows)
    col_in = (cols >= 0) & (cols < total_cols)
    return (row_in[:, None] & col_in[None, :])[:, :, None]


def masked_layer(field, kernel, row_start, col_start, total_rows, total_cols):
    out = valid_conv(field, kernel)
    mask = inside_mask(row_start, col_start, out.shape[0], out.shape[1], total_rows, total_cols)
    return jnp.where(mask, jnp.maximum(out, 0.0), 0.0).astype(jnp.bfloat16)


def shards(
    reflectance,
    scene_class,
    quality,
    class_score,
    encode_first,
    encode_second,
    middle_first,
    middle_second,
    decode_kernel,
    head_weight,
):
    block_rows = quality.shape[1]
    block_cols = quality.shape[2]
    total_rows = block_rows * lax.axis_size("row")
    total_cols = block_cols * lax.axis_size("col")
    weights, shift = shifted_weights(class_score, scene_class, quality)
    part_sums = jnp.sum(weights[:, None] * reflectance, axis=0)
    part_total = jnp.sum(weights, axis=0)
    packed = jnp.concatenate([part_sums, part_total[None], shift[None]], axis=0).astype(jnp.bfloat16)
    gathered = lax.all_gather(packed, "tm", axis=0).astype(jnp.float32)
    shifts = gathered[:, -1]
    scale = jnp.exp(shifts - jnp.max(shifts, axis=0)[None])
    band_sums = jnp.sum(scale[:, None] * gathered[:, :-2], axis=0)
    total_weight = jnp.sum(scale * gathered[:, -2], axis=0)
    composite = (band_sums / total_weight[None]).astype(jnp.bfloat16)

    row0 = lax.axis_index("row") * block_rows
    col0 = lax.axis_index("col") * block_cols
    widened = with_halo(composite.transpose(1, 2, 0), (("row", 0), ("col", 1)), HALO)
    first_map = masked_layer(widened, encode_first, row0 - HALO + 1, col0 - HALO + 1, total_rows, total_cols)
    skip_wide = masked_layer(first_map, encode_second, row0 - HALO + 2, col0 - HALO + 2, total_rows, total_cols)
    wide_rows, wide_cols, channels = skip_wide.shape
    col_pairs = jnp.einsum(
        "vw,hwc->hvc", pair_matrix(wide_cols // 2, wide_cols, 0), skip_wide, preferred_element_type=jnp.float32
    )
    pooled = (
        jnp.sum(col_pairs.reshape(wide_rows // 2, 2, wide_cols // 2, channels), axis=1) * 0.25
    ).astype(jnp.bfloat16)
    coarse_halo = (HALO - 2) // 2
    crow0 = row0 // 2 - coarse_halo
    ccol0 = col0 // 2 - coarse_halo
    mid = masked_layer(pooled, middle_first, crow0 + 1, ccol0 + 1, total_rows // 2, total_cols // 2)
    deeper = masked_layer(mid, middle_second, crow0 + 2, ccol0 + 2, total_rows // 2, total_cols // 2)
    up_halo = 2 * (coarse_halo - 2)
    deep_rows, deep_cols, deep_ch = deeper.shape
    spread = jnp.einsum(
        "wv,hvc->hwc",
        pair_matrix(deep_cols, block_cols + 2, up_halo - 1).T,
        deeper,
        preferred_element_type=jnp.float32,
    ).astype(jnp.bfloat16)
    upsampled = jnp.broadcast_to(spread[:, None], (deep_rows, 2, block_cols + 2, deep_ch)).reshape(
        2 * deep_rows, block_cols + 2, deep_ch
    )[up_halo - 1 : up_halo + block_rows + 1]
    skip_halo = HALO - 2
    skip = skip_wide[skip_halo - 1 : skip_halo + block_rows + 1, skip_halo - 1 : skip_halo + block_cols + 1]
    joined = jnp.concatenate([skip, upsampled], axis=2)
    decoded = jnp.maximum(valid_conv(joined, decode_kernel), 0.0).astype(jnp.bfloat16)
    return jnp.einsum(
        "oc,hwc->ohw", head_weight, decoded, preferred_element_type=jnp.float32
    ).astype(jnp.bfloat16)


def solution(mesh):
    placed = (
        P("tm", None, "row", "col"),
        P("tm", "row", "col"),
        P("tm", "row", "col"),
        P(),
        P(),
        P(),
        P(),
        P(),
        P(),
        P(),
    )
    return jax.shard_map(
        shards, mesh=mesh, in_specs=placed, out_specs=P(None, "row", "col"), check_vma=False
    )
```

```python
import jax
import jax.numpy as jnp
from jax import lax
from jax.experimental import pallas as pl
from jax.experimental.pallas import tpu as pltpu
from jax.sharding import PartitionSpec as P

HALO = 8


def with_halo(cells, sides, width):
    for axis, dim in sides:
        count = lax.axis_size(axis)
        ends = count - 1
        head = lax.slice_in_dim(cells, 0, width, axis=dim)
        tail = lax.slice_in_dim(cells, cells.shape[dim] - width, cells.shape[dim], axis=dim)
        if count == 2:
            first = lax.axis_index(axis) == 0
            got = lax.ppermute(jnp.where(first, tail, head), axis, [(0, 1), (1, 0)])
            empty = jnp.zeros_like(got)
            cells = jnp.concatenate(
                [jnp.where(first, empty, got), cells, jnp.where(first, got, empty)], axis=dim
            )
            continue
        cells = jnp.concatenate(
            [
                lax.ppermute(tail, axis, [(i, (i + 1) % count) for i in range(ends)]),
                cells,
                lax.ppermute(head, axis, [((i + 1) % count, i) for i in range(ends)]),
            ],
            axis=dim,
        )
    return cells


def valid_conv(padded, kernel):
    taps, _, outs, ins = kernel.shape
    height = padded.shape[0] - taps + 1
    width = padded.shape[1] - taps + 1
    stacked = jnp.stack(
        [padded[a : a + height, e : e + width] for a in range(taps) for e in range(taps)], axis=0
    )
    return jnp.einsum(
        "thwc,toc->hwo", stacked, kernel.reshape(taps * taps, outs, ins), preferred_element_type=jnp.float32
    )


def pair_matrix(narrow, wide, offset):
    pick = (jnp.arange(wide, dtype=jnp.int32) + offset) // 2
    return (jnp.arange(narrow, dtype=jnp.int32)[:, None] == pick[None, :]).astype(jnp.bfloat16)


def weight_kernel(score_ref, class_ref, quality_ref, weight_ref, shift_ref):
    dates, rows, _ = class_ref.shape
    classes = score_ref.shape[0]
    step = 8

    def chunk(index, carry):
        at = pl.ds(pl.multiple_of(index * step, step), step)

        def score(date):
            label = class_ref[date, at, :]
            looked = jnp.zeros(label.shape, jnp.float32)
            for k in range(classes):
                looked = jnp.where(label == k, score_ref[k], looked)
            return looked + quality_ref[date, at, :]

        top = lax.fori_loop(1, dates, lambda date, top: jnp.maximum(top, score(date)), score(0))
        shift = top.astype(jnp.bfloat16).astype(jnp.float32)
        shift_ref[at, :] = shift

        def one_date(date, inner):
            weight_ref[date, at, :] = jnp.exp(score(date) - shift)
            return inner

        lax.fori_loop(0, dates, one_date, 0)
        return carry

    lax.fori_loop(0, rows // step, chunk, 0)


def shifted_weights(class_score, scene_class, quality):
    dates, rows, cols = quality.shape
    vmem = pl.BlockSpec(memory_space=pltpu.VMEM)
    return pl.pallas_call(
        weight_kernel,
        out_shape=(
            jax.ShapeDtypeStruct((dates, rows, cols), jnp.float32),
            jax.ShapeDtypeStruct((rows, cols), jnp.float32),
        ),
        in_specs=[pl.BlockSpec(memory_space=pltpu.SMEM), vmem, vmem],
        out_specs=(vmem, vmem),
    )(class_score, scene_class, quality)


def inside_mask(row_start, col_start, height, width, total_rows, total_cols):
    rows = row_start + jnp.arange(height, dtype=jnp.int32)
    cols = col_start + jnp.arange(width, dtype=jnp.int32)
    row_in = (rows >= 0) & (rows < total_rows)
    col_in = (cols >= 0) & (cols < total_cols)
    return (row_in[:, None] & col_in[None, :])[:, :, None]


def masked_layer(field, kernel, row_start, col_start, total_rows, total_cols):
    out = valid_conv(field, kernel)
    mask = inside_mask(row_start, col_start, out.shape[0], out.shape[1], total_rows, total_cols)
    return jnp.where(mask, jnp.maximum(out, 0.0), 0.0).astype(jnp.bfloat16)


def shards(
    reflectance,
    scene_class,
    quality,
    class_score,
    encode_first,
    encode_second,
    middle_first,
    middle_second,
    decode_kernel,
    head_weight,
):
    block_rows = quality.shape[1]
    block_cols = quality.shape[2]
    total_rows = block_rows * lax.axis_size("row")
    total_cols = block_cols * lax.axis_size("col")
    weights, shift = shifted_weights(class_score, scene_class, quality)
    part_sums = jnp.sum(weights[:, None] * reflectance, axis=0)
    part_total = jnp.sum(weights, axis=0)
    packed = jnp.concatenate([part_sums, part_total[None], shift[None]], axis=0).astype(jnp.bfloat16)
    gathered = lax.all_gather(packed, "tm", axis=0).astype(jnp.float32)
    shifts = gathered[:, -1]
    scale = jnp.exp(shifts - jnp.max(shifts, axis=0)[None])
    band_sums = jnp.sum(scale[:, None] * gathered[:, :-2], axis=0)
    total_weight = jnp.sum(scale * gathered[:, -2], axis=0)
    composite = (band_sums / total_weight[None]).astype(jnp.bfloat16)

    row0 = lax.axis_index("row") * block_rows
    col0 = lax.axis_index("col") * block_cols
    widened = with_halo(composite.transpose(1, 2, 0), (("row", 0), ("col", 1)), HALO)
    first_map = masked_layer(widened, encode_first, row0 - HALO + 1, col0 - HALO + 1, total_rows, total_cols)
    skip_wide = masked_layer(first_map, encode_second, row0 - HALO + 2, col0 - HALO + 2, total_rows, total_cols)
    wide_rows, wide_cols, channels = skip_wide.shape
    col_pairs = jnp.einsum(
        "vw,hwc->hvc", pair_matrix(wide_cols // 2, wide_cols, 0), skip_wide, preferred_element_type=jnp.float32
    )
    pooled = (
        jnp.sum(col_pairs.reshape(wide_rows // 2, 2, wide_cols // 2, channels), axis=1) * 0.25
    ).astype(jnp.bfloat16)
    coarse_halo = (HALO - 2) // 2
    crow0 = row0 // 2 - coarse_halo
    ccol0 = col0 // 2 - coarse_halo
    mid = masked_layer(pooled, middle_first, crow0 + 1, ccol0 + 1, total_rows // 2, total_cols // 2)
    deeper = masked_layer(mid, middle_second, crow0 + 2, ccol0 + 2, total_rows // 2, total_cols // 2)
    up_halo = 2 * (coarse_halo - 2)
    deep_rows, deep_cols, deep_ch = deeper.shape
    spread = jnp.einsum(
        "wv,hvc->hwc",
        pair_matrix(deep_cols, block_cols + 2, up_halo - 1).T,
        deeper,
        preferred_element_type=jnp.float32,
    ).astype(jnp.bfloat16)
    upsampled = jnp.broadcast_to(spread[:, None], (deep_rows, 2, block_cols + 2, deep_ch)).reshape(
        2 * deep_rows, block_cols + 2, deep_ch
    )[up_halo - 1 : up_halo + block_rows + 1]
    skip_halo = HALO - 2
    skip = skip_wide[skip_halo - 1 : skip_halo + block_rows + 1, skip_halo - 1 : skip_halo + block_cols + 1]
    joined = jnp.concatenate([skip, upsampled], axis=2)
    decoded = jnp.maximum(valid_conv(joined, decode_kernel), 0.0).astype(jnp.bfloat16)
    return jnp.einsum(
        "oc,hwc->ohw", head_weight, decoded, preferred_element_type=jnp.float32
    ).astype(jnp.bfloat16)


def solution(mesh):
    placed = (
        P("tm", None, "row", "col"),
        P("tm", "row", "col"),
        P("tm", "row", "col"),
        P(),
        P(),
        P(),
        P(),
        P(),
        P(),
        P(),
    )
    return jax.shard_map(
        shards, mesh=mesh, in_specs=placed, out_specs=P(None, "row", "col"), check_vma=False
    )
```

```python
import jax
import jax.numpy as jnp
from jax import lax
from jax.experimental import pallas as pl
from jax.experimental.pallas import tpu as pltpu
from jax.sharding import PartitionSpec as P

HALO = 8


def with_halo(cells, sides, width):
    for axis, dim in sides:
        count = lax.axis_size(axis)
        ends = count - 1
        head = lax.slice_in_dim(cells, 0, width, axis=dim)
        tail = lax.slice_in_dim(cells, cells.shape[dim] - width, cells.shape[dim], axis=dim)
        if count == 2:
            first = lax.axis_index(axis) == 0
            got = lax.ppermute(jnp.where(first, tail, head), axis, [(0, 1), (1, 0)])
            empty = jnp.zeros_like(got)
            cells = jnp.concatenate(
                [jnp.where(first, empty, got), cells, jnp.where(first, got, empty)], axis=dim
            )
            continue
        cells = jnp.concatenate(
            [
                lax.ppermute(tail, axis, [(i, (i + 1) % count) for i in range(ends)]),
                cells,
                lax.ppermute(head, axis, [((i + 1) % count, i) for i in range(ends)]),
            ],
            axis=dim,
        )
    return cells


def valid_conv(padded, kernel):
    taps = kernel.shape[0]
    height = padded.shape[0] - taps + 1
    width = padded.shape[1] - taps + 1
    total = None
    for a in range(taps):
        for e in range(taps):
            term = jnp.einsum(
                "hwc,oc->hwo",
                padded[a : a + height, e : e + width],
                kernel[a, e],
                preferred_element_type=jnp.float32,
            )
            total = term if total is None else total + term
    return total


def pair_matrix(narrow, wide, offset):
    pick = (jnp.arange(wide, dtype=jnp.int32) + offset) // 2
    return (jnp.arange(narrow, dtype=jnp.int32)[:, None] == pick[None, :]).astype(jnp.bfloat16)


def weight_kernel(score_ref, class_ref, quality_ref, weight_ref, shift_ref):
    dates, rows, _ = class_ref.shape
    classes = score_ref.shape[0]
    step = 16

    def chunk(index, carry):
        at = pl.ds(pl.multiple_of(index * step, step), step)

        def score(date, top):
            label = class_ref[date, at, :]
            looked = jnp.zeros(label.shape, jnp.float32)
            for k in range(classes):
                looked = jnp.where(label == k, score_ref[k], looked)
            value = looked + quality_ref[date, at, :]
            weight_ref[date, at, :] = value
            return jnp.maximum(top, value)

        start = jnp.full((step, weight_ref.shape[2]), -jnp.inf, jnp.float32)
        top = lax.fori_loop(0, dates, score, start)
        shift = top.astype(jnp.bfloat16).astype(jnp.float32)
        shift_ref[at, :] = shift

        def one_date(date, inner):
            weight_ref[date, at, :] = jnp.exp(weight_ref[date, at, :] - shift)
            return inner

        lax.fori_loop(0, dates, one_date, 0)
        return carry

    lax.fori_loop(0, rows // step, chunk, 0)


def shifted_weights(class_score, scene_class, quality):
    dates, rows, cols = quality.shape
    vmem = pl.BlockSpec(memory_space=pltpu.VMEM)
    return pl.pallas_call(
        weight_kernel,
        out_shape=(
            jax.ShapeDtypeStruct((dates, rows, cols), jnp.float32),
            jax.ShapeDtypeStruct((rows, cols), jnp.float32),
        ),
        in_specs=[pl.BlockSpec(memory_space=pltpu.SMEM), vmem, vmem],
        out_specs=(vmem, vmem),
    )(class_score, scene_class, quality)


def inside_mask(row_start, col_start, height, width, total_rows, total_cols):
    rows = row_start + jnp.arange(height, dtype=jnp.int32)
    cols = col_start + jnp.arange(width, dtype=jnp.int32)
    row_in = (rows >= 0) & (rows < total_rows)
    col_in = (cols >= 0) & (cols < total_cols)
    return (row_in[:, None] & col_in[None, :])[:, :, None]


def masked_layer(field, kernel, row_start, col_start, total_rows, total_cols):
    out = valid_conv(field, kernel)
    mask = inside_mask(row_start, col_start, out.shape[0], out.shape[1], total_rows, total_cols)
    return jnp.where(mask, jnp.maximum(out, 0.0), 0.0).astype(jnp.bfloat16)


def shards(
    reflectance,
    scene_class,
    quality,
    class_score,
    encode_first,
    encode_second,
    middle_first,
    middle_second,
    decode_kernel,
    head_weight,
):
    block_rows = quality.shape[1]
    block_cols = quality.shape[2]
    total_rows = block_rows * lax.axis_size("row")
    total_cols = block_cols * lax.axis_size("col")
    weights, shift = shifted_weights(class_score, scene_class, quality)
    part_sums = jnp.sum(weights[:, None] * reflectance, axis=0)
    part_total = jnp.sum(weights, axis=0)
    packed = jnp.concatenate([part_sums, part_total[None], shift[None]], axis=0).astype(jnp.bfloat16)
    gathered = lax.all_gather(packed, "tm", axis=0).astype(jnp.float32)
    shifts = gathered[:, -1]
    scale = jnp.exp(shifts - jnp.max(shifts, axis=0)[None])
    band_sums = jnp.sum(scale[:, None] * gathered[:, :-2], axis=0)
    total_weight = jnp.sum(scale * gathered[:, -2], axis=0)
    composite = (band_sums / total_weight[None]).astype(jnp.bfloat16)

    row0 = lax.axis_index("row") * block_rows
    col0 = lax.axis_index("col") * block_cols
    widened = with_halo(composite.transpose(1, 2, 0), (("row", 0), ("col", 1)), HALO)
    first_map = masked_layer(widened, encode_first, row0 - HALO + 1, col0 - HALO + 1, total_rows, total_cols)
    skip_wide = masked_layer(first_map, encode_second, row0 - HALO + 2, col0 - HALO + 2, total_rows, total_cols)
    wide_rows, wide_cols, channels = skip_wide.shape
    col_pairs = jnp.einsum(
        "vw,hwc->hvc", pair_matrix(wide_cols // 2, wide_cols, 0), skip_wide, preferred_element_type=jnp.float32
    )
    pooled = (
        jnp.sum(col_pairs.reshape(wide_rows // 2, 2, wide_cols // 2, channels), axis=1) * 0.25
    ).astype(jnp.bfloat16)
    coarse_halo = (HALO - 2) // 2
    crow0 = row0 // 2 - coarse_halo
    ccol0 = col0 // 2 - coarse_halo
    mid = masked_layer(pooled, middle_first, crow0 + 1, ccol0 + 1, total_rows // 2, total_cols // 2)
    deeper = masked_layer(mid, middle_second, crow0 + 2, ccol0 + 2, total_rows // 2, total_cols // 2)
    up_halo = 2 * (coarse_halo - 2)
    deep_rows, deep_cols, deep_ch = deeper.shape
    spread = jnp.einsum(
        "wv,hvc->hwc",
        pair_matrix(deep_cols, block_cols + 2, up_halo - 1).T,
        deeper,
        preferred_element_type=jnp.float32,
    ).astype(jnp.bfloat16)
    upsampled = jnp.broadcast_to(spread[:, None], (deep_rows, 2, block_cols + 2, deep_ch)).reshape(
        2 * deep_rows, block_cols + 2, deep_ch
    )[up_halo - 1 : up_halo + block_rows + 1]
    skip_halo = HALO - 2
    skip = skip_wide[skip_halo - 1 : skip_halo + block_rows + 1, skip_halo - 1 : skip_halo + block_cols + 1]
    joined = jnp.concatenate([skip, upsampled], axis=2)
    decoded = jnp.maximum(valid_conv(joined, decode_kernel), 0.0).astype(jnp.bfloat16)
    return jnp.einsum(
        "oc,hwc->ohw", head_weight, decoded, preferred_element_type=jnp.float32
    ).astype(jnp.bfloat16)


def solution(mesh):
    placed = (
        P("tm", None, "row", "col"),
        P("tm", "row", "col"),
        P("tm", "row", "col"),
        P(),
        P(),
        P(),
        P(),
        P(),
        P(),
        P(),
    )
    return jax.shard_map(
        shards, mesh=mesh, in_specs=placed, out_specs=P(None, "row", "col"), check_vma=False
    )
```

```python
import jax
import jax.numpy as jnp
from jax import lax
from jax.experimental import pallas as pl
from jax.experimental.pallas import tpu as pltpu
from jax.sharding import PartitionSpec as P

HALO = 8


def with_halo(cells, sides, width):
    for axis, dim in sides:
        count = lax.axis_size(axis)
        ends = count - 1
        head = lax.slice_in_dim(cells, 0, width, axis=dim)
        tail = lax.slice_in_dim(cells, cells.shape[dim] - width, cells.shape[dim], axis=dim)
        if count == 2:
            first = lax.axis_index(axis) == 0
            got = lax.ppermute(jnp.where(first, tail, head), axis, [(0, 1), (1, 0)])
            empty = jnp.zeros_like(got)
            cells = jnp.concatenate(
                [jnp.where(first, empty, got), cells, jnp.where(first, got, empty)], axis=dim
            )
            continue
        cells = jnp.concatenate(
            [
                lax.ppermute(tail, axis, [(i, (i + 1) % count) for i in range(ends)]),
                cells,
                lax.ppermute(head, axis, [((i + 1) % count, i) for i in range(ends)]),
            ],
            axis=dim,
        )
    return cells


def valid_conv(padded, kernel):
    taps = kernel.shape[0]
    height = padded.shape[0] - taps + 1
    width = padded.shape[1] - taps + 1
    total = None
    for a in range(taps):
        for e in range(taps):
            term = jnp.einsum(
                "hwc,oc->hwo",
                padded[a : a + height, e : e + width],
                kernel[a, e],
                preferred_element_type=jnp.float32,
            )
            total = term if total is None else total + term
    return total


def native_conv(padded, kernel):
    return lax.conv_general_dilated(
        padded[None],
        kernel,
        (1, 1),
        "VALID",
        dimension_numbers=("NHWC", "HWOI", "NHWC"),
        preferred_element_type=jnp.float32,
    )[0]


def pair_matrix(narrow, wide, offset):
    pick = (jnp.arange(wide, dtype=jnp.int32) + offset) // 2
    return (jnp.arange(narrow, dtype=jnp.int32)[:, None] == pick[None, :]).astype(jnp.bfloat16)


def weight_kernel(score_ref, class_ref, quality_ref, weight_ref, shift_ref):
    dates, rows, _ = class_ref.shape
    classes = score_ref.shape[0]
    step = 16

    def chunk(index, carry):
        at = pl.ds(pl.multiple_of(index * step, step), step)

        def score(date, top):
            label = class_ref[date, at, :]
            looked = jnp.zeros(label.shape, jnp.float32)
            for k in range(classes):
                looked = jnp.where(label == k, score_ref[k], looked)
            value = looked + quality_ref[date, at, :]
            weight_ref[date, at, :] = value
            return jnp.maximum(top, value)

        start = jnp.full((step, weight_ref.shape[2]), -jnp.inf, jnp.float32)
        top = lax.fori_loop(0, dates, score, start)
        shift = top.astype(jnp.bfloat16).astype(jnp.float32)
        shift_ref[at, :] = shift

        def one_date(date, inner):
            weight_ref[date, at, :] = jnp.exp(weight_ref[date, at, :] - shift)
            return inner

        lax.fori_loop(0, dates, one_date, 0)
        return carry

    lax.fori_loop(0, rows // step, chunk, 0)


def shifted_weights(class_score, scene_class, quality):
    dates, rows, cols = quality.shape
    vmem = pl.BlockSpec(memory_space=pltpu.VMEM)
    return pl.pallas_call(
        weight_kernel,
        out_shape=(
            jax.ShapeDtypeStruct((dates, rows, cols), jnp.float32),
            jax.ShapeDtypeStruct((rows, cols), jnp.float32),
        ),
        in_specs=[pl.BlockSpec(memory_space=pltpu.SMEM), vmem, vmem],
        out_specs=(vmem, vmem),
    )(class_score, scene_class, quality)


def inside_mask(row_start, col_start, height, width, total_rows, total_cols):
    rows = row_start + jnp.arange(height, dtype=jnp.int32)
    cols = col_start + jnp.arange(width, dtype=jnp.int32)
    row_in = (rows >= 0) & (rows < total_rows)
    col_in = (cols >= 0) & (cols < total_cols)
    return (row_in[:, None] & col_in[None, :])[:, :, None]


def masked_layer(field, kernel, row_start, col_start, total_rows, total_cols, conv=valid_conv):
    out = conv(field, kernel)
    mask = inside_mask(row_start, col_start, out.shape[0], out.shape[1], total_rows, total_cols)
    return jnp.where(mask, jnp.maximum(out, 0.0), 0.0).astype(jnp.bfloat16)


def shards(
    reflectance,
    scene_class,
    quality,
    class_score,
    encode_first,
    encode_second,
    middle_first,
    middle_second,
    decode_kernel,
    head_weight,
):
    block_rows = quality.shape[1]
    block_cols = quality.shape[2]
    total_rows = block_rows * lax.axis_size("row")
    total_cols = block_cols * lax.axis_size("col")
    weights, shift = shifted_weights(class_score, scene_class, quality)
    part_sums = jnp.sum(weights[:, None] * reflectance, axis=0)
    part_total = jnp.sum(weights, axis=0)
    packed = jnp.concatenate([part_sums, part_total[None], shift[None]], axis=0).astype(jnp.bfloat16)
    gathered = lax.all_gather(packed, "tm", axis=0).astype(jnp.float32)
    shifts = gathered[:, -1]
    scale = jnp.exp(shifts - jnp.max(shifts, axis=0)[None])
    band_sums = jnp.sum(scale[:, None] * gathered[:, :-2], axis=0)
    total_weight = jnp.sum(scale * gathered[:, -2], axis=0)
    composite = (band_sums / total_weight[None]).astype(jnp.bfloat16)

    row0 = lax.axis_index("row") * block_rows
    col0 = lax.axis_index("col") * block_cols
    widened = with_halo(composite.transpose(1, 2, 0), (("row", 0), ("col", 1)), HALO)
    first_map = masked_layer(widened, encode_first, row0 - HALO + 1, col0 - HALO + 1, total_rows, total_cols)
    skip_wide = masked_layer(first_map, encode_second, row0 - HALO + 2, col0 - HALO + 2, total_rows, total_cols)
    wide_rows, wide_cols, channels = skip_wide.shape
    col_pairs = jnp.einsum(
        "vw,hwc->hvc", pair_matrix(wide_cols // 2, wide_cols, 0), skip_wide, preferred_element_type=jnp.float32
    )
    pooled = (
        jnp.sum(col_pairs.reshape(wide_rows // 2, 2, wide_cols // 2, channels), axis=1) * 0.25
    ).astype(jnp.bfloat16)
    coarse_halo = (HALO - 2) // 2
    crow0 = row0 // 2 - coarse_halo
    ccol0 = col0 // 2 - coarse_halo
    coarse = (total_rows // 2, total_cols // 2, native_conv)
    mid = masked_layer(pooled, middle_first, crow0 + 1, ccol0 + 1, *coarse)
    deeper = masked_layer(mid, middle_second, crow0 + 2, ccol0 + 2, *coarse)
    up_halo = 2 * (coarse_halo - 2)
    deep_rows, deep_cols, deep_ch = deeper.shape
    spread = jnp.einsum(
        "wv,hvc->hwc",
        pair_matrix(deep_cols, block_cols + 2, up_halo - 1).T,
        deeper,
        preferred_element_type=jnp.float32,
    ).astype(jnp.bfloat16)
    upsampled = jnp.broadcast_to(spread[:, None], (deep_rows, 2, block_cols + 2, deep_ch)).reshape(
        2 * deep_rows, block_cols + 2, deep_ch
    )[up_halo - 1 : up_halo + block_rows + 1]
    skip_halo = HALO - 2
    skip = skip_wide[skip_halo - 1 : skip_halo + block_rows + 1, skip_halo - 1 : skip_halo + block_cols + 1]
    joined = jnp.concatenate([skip, upsampled], axis=2)
    decoded = jnp.maximum(valid_conv(joined, decode_kernel), 0.0).astype(jnp.bfloat16)
    return jnp.einsum(
        "oc,hwc->ohw", head_weight, decoded, preferred_element_type=jnp.float32
    ).astype(jnp.bfloat16)


def solution(mesh):
    placed = (
        P("tm", None, "row", "col"),
        P("tm", "row", "col"),
        P("tm", "row", "col"),
        P(),
        P(),
        P(),
        P(),
        P(),
        P(),
        P(),
    )
    return jax.shard_map(
        shards, mesh=mesh, in_specs=placed, out_specs=P(None, "row", "col"), check_vma=False
    )
```

```python
import jax
import jax.numpy as jnp
from jax import lax
from jax.experimental import pallas as pl
from jax.experimental.pallas import tpu as pltpu
from jax.sharding import PartitionSpec as P

HALO = 8


def with_halo(cells, sides, width):
    for axis, dim in sides:
        count = lax.axis_size(axis)
        ends = count - 1
        head = lax.slice_in_dim(cells, 0, width, axis=dim)
        tail = lax.slice_in_dim(cells, cells.shape[dim] - width, cells.shape[dim], axis=dim)
        if count == 2:
            first = lax.axis_index(axis) == 0
            got = lax.ppermute(jnp.where(first, tail, head), axis, [(0, 1), (1, 0)])
            empty = jnp.zeros_like(got)
            cells = jnp.concatenate(
                [jnp.where(first, empty, got), cells, jnp.where(first, got, empty)], axis=dim
            )
            continue
        cells = jnp.concatenate(
            [
                lax.ppermute(tail, axis, [(i, (i + 1) % count) for i in range(ends)]),
                cells,
                lax.ppermute(head, axis, [((i + 1) % count, i) for i in range(ends)]),
            ],
            axis=dim,
        )
    return cells


def valid_conv(padded, kernel):
    taps = kernel.shape[0]
    height = padded.shape[0] - taps + 1
    width = padded.shape[1] - taps + 1
    total = None
    for a in range(taps):
        for e in range(taps):
            term = jnp.einsum(
                "hwc,oc->hwo",
                padded[a : a + height, e : e + width],
                kernel[a, e],
                preferred_element_type=jnp.float32,
            )
            total = term if total is None else total + term
    return total


def native_conv(padded, kernel):
    return lax.conv_general_dilated(
        padded[None],
        kernel,
        (1, 1),
        "VALID",
        dimension_numbers=("NHWC", "HWOI", "NHWC"),
        preferred_element_type=jnp.float32,
    )[0]


def pair_matrix(narrow, wide, offset):
    pick = (jnp.arange(wide, dtype=jnp.int32) + offset) // 2
    return (jnp.arange(narrow, dtype=jnp.int32)[:, None] == pick[None, :]).astype(jnp.bfloat16)


def weight_kernel(score_ref, class_ref, quality_ref, weight_ref, shift_ref):
    dates, rows, _ = class_ref.shape
    classes = score_ref.shape[0]
    step = 16

    def chunk(index, carry):
        at = pl.ds(pl.multiple_of(index * step, step), step)

        def score(date, top):
            label = class_ref[date, at, :]
            looked = jnp.zeros(label.shape, jnp.float32)
            for k in range(classes):
                looked = jnp.where(label == k, score_ref[k], looked)
            value = looked + quality_ref[date, at, :]
            weight_ref[date, at, :] = value
            return jnp.maximum(top, value)

        start = jnp.full((step, weight_ref.shape[2]), -jnp.inf, jnp.float32)
        top = lax.fori_loop(0, dates, score, start)
        shift = top.astype(jnp.bfloat16).astype(jnp.float32)
        shift_ref[at, :] = shift

        def one_date(date, inner):
            weight_ref[date, at, :] = jnp.exp(weight_ref[date, at, :] - shift)
            return inner

        lax.fori_loop(0, dates, one_date, 0)
        return carry

    lax.fori_loop(0, rows // step, chunk, 0)


def shifted_weights(class_score, scene_class, quality):
    dates, rows, cols = quality.shape
    vmem = pl.BlockSpec(memory_space=pltpu.VMEM)
    return pl.pallas_call(
        weight_kernel,
        out_shape=(
            jax.ShapeDtypeStruct((dates, rows, cols), jnp.float32),
            jax.ShapeDtypeStruct((rows, cols), jnp.float32),
        ),
        in_specs=[pl.BlockSpec(memory_space=pltpu.SMEM), vmem, vmem],
        out_specs=(vmem, vmem),
    )(class_score, scene_class, quality)


def inside_mask(row_start, col_start, height, width, total_rows, total_cols):
    rows = row_start + jnp.arange(height, dtype=jnp.int32)
    cols = col_start + jnp.arange(width, dtype=jnp.int32)
    row_in = (rows >= 0) & (rows < total_rows)
    col_in = (cols >= 0) & (cols < total_cols)
    return (row_in[:, None] & col_in[None, :])[:, :, None]


def masked_layer(field, kernel, row_start, col_start, total_rows, total_cols, conv=valid_conv):
    out = conv(field, kernel)
    mask = inside_mask(row_start, col_start, out.shape[0], out.shape[1], total_rows, total_cols)
    return jnp.where(mask, jnp.maximum(out, 0.0), 0.0).astype(jnp.bfloat16)


def shards(
    reflectance,
    scene_class,
    quality,
    class_score,
    encode_first,
    encode_second,
    middle_first,
    middle_second,
    decode_kernel,
    head_weight,
):
    block_rows = quality.shape[1]
    block_cols = quality.shape[2]
    total_rows = block_rows * lax.axis_size("row")
    total_cols = block_cols * lax.axis_size("col")
    weights, shift = shifted_weights(class_score, scene_class, quality)
    part_sums = jnp.sum(weights[:, None] * reflectance, axis=0)
    part_total = jnp.sum(weights, axis=0)
    packed = jnp.concatenate([part_sums, part_total[None], shift[None]], axis=0).astype(jnp.bfloat16)
    def combine(part):
        gathered = lax.all_gather(part, "tm", axis=0).astype(jnp.float32)
        shifts = gathered[:, -1]
        scale = jnp.exp(shifts - jnp.max(shifts, axis=0)[None])
        band_sums = jnp.sum(scale[:, None] * gathered[:, :-2], axis=0)
        total_weight = jnp.sum(scale * gathered[:, -2], axis=0)
        return (band_sums / total_weight[None]).astype(jnp.bfloat16).transpose(1, 2, 0)

    half = block_rows // 2
    upper = combine(packed[:, :half])
    ends = lax.axis_size("row") - 1
    from_below = lax.ppermute(upper[:HALO], "row", [(i + 1, i) for i in range(ends)])
    lower = combine(packed[:, half:])
    from_above = lax.ppermute(lower[half - HALO :], "row", [(i, i + 1) for i in range(ends)])
    stacked = jnp.concatenate([from_above, upper, lower, from_below], axis=0)

    row0 = lax.axis_index("row") * block_rows
    col0 = lax.axis_index("col") * block_cols
    widened = with_halo(stacked, (("col", 1),), HALO)
    first_map = masked_layer(widened, encode_first, row0 - HALO + 1, col0 - HALO + 1, total_rows, total_cols)
    skip_wide = masked_layer(first_map, encode_second, row0 - HALO + 2, col0 - HALO + 2, total_rows, total_cols)
    wide_rows, wide_cols, channels = skip_wide.shape
    col_pairs = jnp.einsum(
        "vw,hwc->hvc", pair_matrix(wide_cols // 2, wide_cols, 0), skip_wide, preferred_element_type=jnp.float32
    )
    pooled = (
        jnp.sum(col_pairs.reshape(wide_rows // 2, 2, wide_cols // 2, channels), axis=1) * 0.25
    ).astype(jnp.bfloat16)
    coarse_halo = (HALO - 2) // 2
    crow0 = row0 // 2 - coarse_halo
    ccol0 = col0 // 2 - coarse_halo
    coarse = (total_rows // 2, total_cols // 2, native_conv)
    mid = masked_layer(pooled, middle_first, crow0 + 1, ccol0 + 1, *coarse)
    deeper = masked_layer(mid, middle_second, crow0 + 2, ccol0 + 2, *coarse)
    up_halo = 2 * (coarse_halo - 2)
    deep_rows, deep_cols, deep_ch = deeper.shape
    spread = jnp.einsum(
        "wv,hvc->hwc",
        pair_matrix(deep_cols, block_cols + 2, up_halo - 1).T,
        deeper,
        preferred_element_type=jnp.float32,
    ).astype(jnp.bfloat16)
    upsampled = jnp.broadcast_to(spread[:, None], (deep_rows, 2, block_cols + 2, deep_ch)).reshape(
        2 * deep_rows, block_cols + 2, deep_ch
    )[up_halo - 1 : up_halo + block_rows + 1]
    skip_halo = HALO - 2
    skip = skip_wide[skip_halo - 1 : skip_halo + block_rows + 1, skip_halo - 1 : skip_halo + block_cols + 1]
    joined = jnp.concatenate([skip, upsampled], axis=2)
    decoded = jnp.maximum(valid_conv(joined, decode_kernel), 0.0).astype(jnp.bfloat16)
    return jnp.einsum(
        "oc,hwc->ohw", head_weight, decoded, preferred_element_type=jnp.float32
    ).astype(jnp.bfloat16)


def solution(mesh):
    placed = (
        P("tm", None, "row", "col"),
        P("tm", "row", "col"),
        P("tm", "row", "col"),
        P(),
        P(),
        P(),
        P(),
        P(),
        P(),
        P(),
    )
    return jax.shard_map(
        shards, mesh=mesh, in_specs=placed, out_specs=P(None, "row", "col"), check_vma=False
    )
```

```python
import jax
import jax.numpy as jnp
from jax import lax
from jax.experimental import pallas as pl
from jax.experimental.pallas import tpu as pltpu
from jax.sharding import PartitionSpec as P

HALO = 8


def with_halo(cells, sides, width):
    for axis, dim in sides:
        count = lax.axis_size(axis)
        ends = count - 1
        head = lax.slice_in_dim(cells, 0, width, axis=dim)
        tail = lax.slice_in_dim(cells, cells.shape[dim] - width, cells.shape[dim], axis=dim)
        if count == 2:
            first = lax.axis_index(axis) == 0
            got = lax.ppermute(jnp.where(first, tail, head), axis, [(0, 1), (1, 0)])
            empty = jnp.zeros_like(got)
            cells = jnp.concatenate(
                [jnp.where(first, empty, got), cells, jnp.where(first, got, empty)], axis=dim
            )
            continue
        cells = jnp.concatenate(
            [
                lax.ppermute(tail, axis, [(i, (i + 1) % count) for i in range(ends)]),
                cells,
                lax.ppermute(head, axis, [((i + 1) % count, i) for i in range(ends)]),
            ],
            axis=dim,
        )
    return cells


def valid_conv(padded, kernel):
    taps = kernel.shape[0]
    height = padded.shape[0] - taps + 1
    width = padded.shape[1] - taps + 1
    total = None
    for a in range(taps):
        for e in range(taps):
            term = jnp.einsum(
                "hwc,oc->hwo",
                padded[a : a + height, e : e + width],
                kernel[a, e],
                preferred_element_type=jnp.float32,
            )
            total = term if total is None else total + term
    return total


def native_conv(padded, kernel):
    return lax.conv_general_dilated(
        padded[None],
        kernel,
        (1, 1),
        "VALID",
        dimension_numbers=("NHWC", "HWOI", "NHWC"),
        preferred_element_type=jnp.float32,
    )[0]


def pair_matrix(narrow, wide, offset):
    pick = (jnp.arange(wide, dtype=jnp.int32) + offset) // 2
    return (jnp.arange(narrow, dtype=jnp.int32)[:, None] == pick[None, :]).astype(jnp.bfloat16)


def weight_kernel(score_ref, class_ref, quality_ref, weight_ref, shift_ref):
    dates, rows, _ = class_ref.shape
    classes = score_ref.shape[0]
    step = 16

    def chunk(index, carry):
        at = pl.ds(pl.multiple_of(index * step, step), step)

        def score(date, top):
            label = class_ref[date, at, :]
            looked = jnp.zeros(label.shape, jnp.float32)
            for k in range(classes):
                looked = jnp.where(label == k, score_ref[k], looked)
            value = looked + quality_ref[date, at, :]
            weight_ref[date, at, :] = value
            return jnp.maximum(top, value)

        start = jnp.full((step, weight_ref.shape[2]), -jnp.inf, jnp.float32)
        top = lax.fori_loop(0, dates, score, start)
        shift = top.astype(jnp.bfloat16).astype(jnp.float32)
        shift_ref[at, :] = shift

        def one_date(date, inner):
            weight_ref[date, at, :] = jnp.exp(weight_ref[date, at, :] - shift)
            return inner

        lax.fori_loop(0, dates, one_date, 0)
        return carry

    lax.fori_loop(0, rows // step, chunk, 0)


def shifted_weights(class_score, scene_class, quality):
    dates, rows, cols = quality.shape
    vmem = pl.BlockSpec(memory_space=pltpu.VMEM)
    return pl.pallas_call(
        weight_kernel,
        out_shape=(
            jax.ShapeDtypeStruct((dates, rows, cols), jnp.float32),
            jax.ShapeDtypeStruct((rows, cols), jnp.float32),
        ),
        in_specs=[pl.BlockSpec(memory_space=pltpu.SMEM), vmem, vmem],
        out_specs=(vmem, vmem),
    )(class_score, scene_class, quality)


def inside_mask(row_start, col_start, height, width, total_rows, total_cols):
    rows = row_start + jnp.arange(height, dtype=jnp.int32)
    cols = col_start + jnp.arange(width, dtype=jnp.int32)
    row_in = (rows >= 0) & (rows < total_rows)
    col_in = (cols >= 0) & (cols < total_cols)
    return (row_in[:, None] & col_in[None, :])[:, :, None]


def masked_layer(field, kernel, row_start, col_start, total_rows, total_cols, conv=valid_conv):
    out = conv(field, kernel)
    mask = inside_mask(row_start, col_start, out.shape[0], out.shape[1], total_rows, total_cols)
    return jnp.where(mask, jnp.maximum(out, 0.0), 0.0).astype(jnp.bfloat16)


def shards(
    reflectance,
    scene_class,
    quality,
    class_score,
    encode_first,
    encode_second,
    middle_first,
    middle_second,
    decode_kernel,
    head_weight,
):
    block_rows = quality.shape[1]
    block_cols = quality.shape[2]
    total_rows = block_rows * lax.axis_size("row")
    total_cols = block_cols * lax.axis_size("col")
    weights, shift = shifted_weights(class_score, scene_class, quality)
    part_sums = jnp.sum(weights[:, None] * reflectance, axis=0)
    part_total = jnp.sum(weights, axis=0)
    packed = jnp.concatenate([part_sums, part_total[None], shift[None]], axis=0).astype(jnp.bfloat16)
    count = lax.axis_size("tm")
    me = lax.axis_index("tm")
    slots = [packed]
    valid = [me >= 0]
    rising = packed
    falling = packed
    for step in range(1, count):
        rising = lax.ppermute(rising, "tm", [(i, i + 1) for i in range(count - 1)])
        falling = lax.ppermute(falling, "tm", [(i + 1, i) for i in range(count - 1)])
        slots += [rising, falling]
        valid += [me - step >= 0, me + step <= count - 1]
    gathered = jnp.stack(slots, axis=0).astype(jnp.float32)
    shifts = jnp.where(jnp.stack(valid)[:, None, None], gathered[:, -1], -jnp.inf)
    scale = jnp.exp(shifts - jnp.max(shifts, axis=0)[None])
    band_sums = jnp.sum(scale[:, None] * gathered[:, :-2], axis=0)
    total_weight = jnp.sum(scale * gathered[:, -2], axis=0)
    composite = (band_sums / total_weight[None]).astype(jnp.bfloat16)

    row0 = lax.axis_index("row") * block_rows
    col0 = lax.axis_index("col") * block_cols
    widened = with_halo(composite.transpose(1, 2, 0), (("row", 0), ("col", 1)), HALO)
    first_map = masked_layer(widened, encode_first, row0 - HALO + 1, col0 - HALO + 1, total_rows, total_cols)
    skip_wide = masked_layer(first_map, encode_second, row0 - HALO + 2, col0 - HALO + 2, total_rows, total_cols)
    wide_rows, wide_cols, channels = skip_wide.shape
    col_pairs = jnp.einsum(
        "vw,hwc->hvc", pair_matrix(wide_cols // 2, wide_cols, 0), skip_wide, preferred_element_type=jnp.float32
    )
    pooled = (
        jnp.sum(col_pairs.reshape(wide_rows // 2, 2, wide_cols // 2, channels), axis=1) * 0.25
    ).astype(jnp.bfloat16)
    coarse_halo = (HALO - 2) // 2
    crow0 = row0 // 2 - coarse_halo
    ccol0 = col0 // 2 - coarse_halo
    coarse = (total_rows // 2, total_cols // 2, native_conv)
    mid = masked_layer(pooled, middle_first, crow0 + 1, ccol0 + 1, *coarse)
    deeper = masked_layer(mid, middle_second, crow0 + 2, ccol0 + 2, *coarse)
    up_halo = 2 * (coarse_halo - 2)
    deep_rows, deep_cols, deep_ch = deeper.shape
    spread = jnp.einsum(
        "wv,hvc->hwc",
        pair_matrix(deep_cols, block_cols + 2, up_halo - 1).T,
        deeper,
        preferred_element_type=jnp.float32,
    ).astype(jnp.bfloat16)
    upsampled = jnp.broadcast_to(spread[:, None], (deep_rows, 2, block_cols + 2, deep_ch)).reshape(
        2 * deep_rows, block_cols + 2, deep_ch
    )[up_halo - 1 : up_halo + block_rows + 1]
    skip_halo = HALO - 2
    skip = skip_wide[skip_halo - 1 : skip_halo + block_rows + 1, skip_halo - 1 : skip_halo + block_cols + 1]
    joined = jnp.concatenate([skip, upsampled], axis=2)
    decoded = jnp.maximum(valid_conv(joined, decode_kernel), 0.0).astype(jnp.bfloat16)
    return jnp.einsum(
        "oc,hwc->ohw", head_weight, decoded, preferred_element_type=jnp.float32
    ).astype(jnp.bfloat16)


def solution(mesh):
    placed = (
        P("tm", None, "row", "col"),
        P("tm", "row", "col"),
        P("tm", "row", "col"),
        P(),
        P(),
        P(),
        P(),
        P(),
        P(),
        P(),
    )
    return jax.shard_map(
        shards, mesh=mesh, in_specs=placed, out_specs=P(None, "row", "col"), check_vma=False
    )
```

```python
import jax
import jax.numpy as jnp
from jax import lax
from jax.experimental import pallas as pl
from jax.experimental.pallas import tpu as pltpu
from jax.sharding import PartitionSpec as P

HALO = 8


def with_halo(cells, sides, width):
    for axis, dim in sides:
        count = lax.axis_size(axis)
        ends = count - 1
        head = lax.slice_in_dim(cells, 0, width, axis=dim)
        tail = lax.slice_in_dim(cells, cells.shape[dim] - width, cells.shape[dim], axis=dim)
        if count == 2:
            first = lax.axis_index(axis) == 0
            got = lax.ppermute(jnp.where(first, tail, head), axis, [(0, 1), (1, 0)])
            empty = jnp.zeros_like(got)
            cells = jnp.concatenate(
                [jnp.where(first, empty, got), cells, jnp.where(first, got, empty)], axis=dim
            )
            continue
        cells = jnp.concatenate(
            [
                lax.ppermute(tail, axis, [(i, (i + 1) % count) for i in range(ends)]),
                cells,
                lax.ppermute(head, axis, [((i + 1) % count, i) for i in range(ends)]),
            ],
            axis=dim,
        )
    return cells


def valid_conv(padded, kernel):
    taps = kernel.shape[0]
    height = padded.shape[0] - taps + 1
    width = padded.shape[1] - taps + 1
    total = None
    for a in range(taps):
        for e in range(taps):
            term = jnp.einsum(
                "hwc,oc->hwo",
                padded[a : a + height, e : e + width],
                kernel[a, e],
                preferred_element_type=jnp.float32,
            )
            total = term if total is None else total + term
    return total


def native_conv(padded, kernel):
    return lax.conv_general_dilated(
        padded[None],
        kernel,
        (1, 1),
        "VALID",
        dimension_numbers=("NHWC", "HWOI", "NHWC"),
        preferred_element_type=jnp.float32,
    )[0]


def pair_matrix(narrow, wide, offset):
    pick = (jnp.arange(wide, dtype=jnp.int32) + offset) // 2
    return (jnp.arange(narrow, dtype=jnp.int32)[:, None] == pick[None, :]).astype(jnp.bfloat16)


def weight_kernel(score_ref, class_ref, quality_ref, weight_ref, shift_ref):
    dates = class_ref.shape[0]
    classes = score_ref.shape[0]

    def score(date, top):
        label = class_ref[date]
        looked = jnp.zeros(label.shape, jnp.float32)
        for k in range(classes):
            looked = jnp.where(label == k, score_ref[k], looked)
        value = looked + quality_ref[date]
        weight_ref[date] = value
        return jnp.maximum(top, value)

    start = jnp.full(shift_ref.shape, -jnp.inf, jnp.float32)
    top = lax.fori_loop(0, dates, score, start)
    shift = top.astype(jnp.bfloat16).astype(jnp.float32)
    shift_ref[...] = shift

    def one_date(date, inner):
        weight_ref[date] = jnp.exp(weight_ref[date] - shift)
        return inner

    lax.fori_loop(0, dates, one_date, 0)


def shifted_weights(class_score, scene_class, quality):
    dates, rows, cols = quality.shape
    step = 8
    planes = pl.BlockSpec((dates, step, cols), lambda i: (0, i, 0))
    return pl.pallas_call(
        weight_kernel,
        out_shape=(
            jax.ShapeDtypeStruct((dates, rows, cols), jnp.float32),
            jax.ShapeDtypeStruct((rows, cols), jnp.float32),
        ),
        grid=(rows // step,),
        in_specs=[pl.BlockSpec(memory_space=pltpu.SMEM), planes, planes],
        out_specs=(planes, pl.BlockSpec((step, cols), lambda i: (i, 0))),
    )(class_score, scene_class, quality)


def inside_mask(row_start, col_start, height, width, total_rows, total_cols):
    rows = row_start + jnp.arange(height, dtype=jnp.int32)
    cols = col_start + jnp.arange(width, dtype=jnp.int32)
    row_in = (rows >= 0) & (rows < total_rows)
    col_in = (cols >= 0) & (cols < total_cols)
    return (row_in[:, None] & col_in[None, :])[:, :, None]


def masked_layer(field, kernel, row_start, col_start, total_rows, total_cols, conv=valid_conv):
    out = conv(field, kernel)
    mask = inside_mask(row_start, col_start, out.shape[0], out.shape[1], total_rows, total_cols)
    return jnp.where(mask, jnp.maximum(out, 0.0), 0.0).astype(jnp.bfloat16)


def shards(
    reflectance,
    scene_class,
    quality,
    class_score,
    encode_first,
    encode_second,
    middle_first,
    middle_second,
    decode_kernel,
    head_weight,
):
    block_rows = quality.shape[1]
    block_cols = quality.shape[2]
    total_rows = block_rows * lax.axis_size("row")
    total_cols = block_cols * lax.axis_size("col")
    weights, shift = shifted_weights(class_score, scene_class, quality)
    part_sums = jnp.sum(weights[:, None] * reflectance, axis=0)
    part_total = jnp.sum(weights, axis=0)
    packed = jnp.concatenate([part_sums, part_total[None], shift[None]], axis=0).astype(jnp.bfloat16)
    gathered = lax.all_gather(packed, "tm", axis=0).astype(jnp.float32)
    shifts = gathered[:, -1]
    scale = jnp.exp(shifts - jnp.max(shifts, axis=0)[None])
    band_sums = jnp.sum(scale[:, None] * gathered[:, :-2], axis=0)
    total_weight = jnp.sum(scale * gathered[:, -2], axis=0)
    composite = (band_sums / total_weight[None]).astype(jnp.bfloat16)

    row0 = lax.axis_index("row") * block_rows
    col0 = lax.axis_index("col") * block_cols
    widened = with_halo(composite.transpose(1, 2, 0), (("row", 0), ("col", 1)), HALO)
    first_map = masked_layer(widened, encode_first, row0 - HALO + 1, col0 - HALO + 1, total_rows, total_cols)
    skip_wide = masked_layer(first_map, encode_second, row0 - HALO + 2, col0 - HALO + 2, total_rows, total_cols)
    wide_rows, wide_cols, channels = skip_wide.shape
    col_pairs = jnp.einsum(
        "vw,hwc->hvc", pair_matrix(wide_cols // 2, wide_cols, 0), skip_wide, preferred_element_type=jnp.float32
    )
    pooled = (
        jnp.sum(col_pairs.reshape(wide_rows // 2, 2, wide_cols // 2, channels), axis=1) * 0.25
    ).astype(jnp.bfloat16)
    coarse_halo = (HALO - 2) // 2
    crow0 = row0 // 2 - coarse_halo
    ccol0 = col0 // 2 - coarse_halo
    coarse = (total_rows // 2, total_cols // 2, native_conv)
    mid = masked_layer(pooled, middle_first, crow0 + 1, ccol0 + 1, *coarse)
    deeper = masked_layer(mid, middle_second, crow0 + 2, ccol0 + 2, *coarse)
    up_halo = 2 * (coarse_halo - 2)
    deep_rows, deep_cols, deep_ch = deeper.shape
    spread = jnp.einsum(
        "wv,hvc->hwc",
        pair_matrix(deep_cols, block_cols + 2, up_halo - 1).T,
        deeper,
        preferred_element_type=jnp.float32,
    ).astype(jnp.bfloat16)
    upsampled = jnp.broadcast_to(spread[:, None], (deep_rows, 2, block_cols + 2, deep_ch)).reshape(
        2 * deep_rows, block_cols + 2, deep_ch
    )[up_halo - 1 : up_halo + block_rows + 1]
    skip_halo = HALO - 2
    skip = skip_wide[skip_halo - 1 : skip_halo + block_rows + 1, skip_halo - 1 : skip_halo + block_cols + 1]
    joined = jnp.concatenate([skip, upsampled], axis=2)
    decoded = jnp.maximum(valid_conv(joined, decode_kernel), 0.0).astype(jnp.bfloat16)
    return jnp.einsum(
        "oc,hwc->ohw", head_weight, decoded, preferred_element_type=jnp.float32
    ).astype(jnp.bfloat16)


def solution(mesh):
    placed = (
        P("tm", None, "row", "col"),
        P("tm", "row", "col"),
        P("tm", "row", "col"),
        P(),
        P(),
        P(),
        P(),
        P(),
        P(),
        P(),
    )
    return jax.shard_map(
        shards, mesh=mesh, in_specs=placed, out_specs=P(None, "row", "col"), check_vma=False
    )
```

```python
import jax
import jax.numpy as jnp
from jax import lax
from jax.experimental import pallas as pl
from jax.experimental.pallas import tpu as pltpu
from jax.sharding import PartitionSpec as P

HALO = 8


def with_halo(cells, sides, width):
    for axis, dim in sides:
        count = lax.axis_size(axis)
        ends = count - 1
        head = lax.slice_in_dim(cells, 0, width, axis=dim)
        tail = lax.slice_in_dim(cells, cells.shape[dim] - width, cells.shape[dim], axis=dim)
        if count == 2:
            first = lax.axis_index(axis) == 0
            got = lax.ppermute(jnp.where(first, tail, head), axis, [(0, 1), (1, 0)])
            empty = jnp.zeros_like(got)
            cells = jnp.concatenate(
                [jnp.where(first, empty, got), cells, jnp.where(first, got, empty)], axis=dim
            )
            continue
        cells = jnp.concatenate(
            [
                lax.ppermute(tail, axis, [(i, (i + 1) % count) for i in range(ends)]),
                cells,
                lax.ppermute(head, axis, [((i + 1) % count, i) for i in range(ends)]),
            ],
            axis=dim,
        )
    return cells


def valid_conv(padded, kernel):
    taps = kernel.shape[0]
    height = padded.shape[0] - taps + 1
    width = padded.shape[1] - taps + 1
    total = None
    for a in range(taps):
        for e in range(taps):
            term = jnp.einsum(
                "hwc,oc->hwo",
                padded[a : a + height, e : e + width],
                kernel[a, e],
                preferred_element_type=jnp.float32,
            )
            total = term if total is None else total + term
    return total


def native_conv(padded, kernel):
    return lax.conv_general_dilated(
        padded[None],
        kernel,
        (1, 1),
        "VALID",
        dimension_numbers=("NHWC", "HWOI", "NHWC"),
        preferred_element_type=jnp.float32,
    )[0]


def pair_matrix(narrow, wide, offset):
    pick = (jnp.arange(wide, dtype=jnp.int32) + offset) // 2
    return (jnp.arange(narrow, dtype=jnp.int32)[:, None] == pick[None, :]).astype(jnp.bfloat16)


def weight_kernel(score_ref, class_ref, quality_ref, weight_ref, shift_ref):
    dates, rows, _ = class_ref.shape
    classes = score_ref.shape[0]
    step = 16

    def chunk(index, carry):
        at = pl.ds(pl.multiple_of(index * step, step), step)

        def score(date, top):
            label = class_ref[date, at, :]
            looked = jnp.zeros(label.shape, jnp.float32)
            for k in range(classes):
                looked = jnp.where(label == k, score_ref[k], looked)
            value = looked + quality_ref[date, at, :]
            weight_ref[date, at, :] = value
            return jnp.maximum(top, value)

        start = jnp.full((step, weight_ref.shape[2]), -jnp.inf, jnp.float32)
        top = lax.fori_loop(0, dates, score, start)
        shift = top.astype(jnp.bfloat16).astype(jnp.float32)
        shift_ref[at, :] = shift

        def one_date(date, inner):
            weight_ref[date, at, :] = jnp.exp(weight_ref[date, at, :] - shift)
            return inner

        lax.fori_loop(0, dates, one_date, 0)
        return carry

    lax.fori_loop(0, rows // step, chunk, 0)


def shifted_weights(class_score, scene_class, quality):
    dates, rows, cols = quality.shape
    vmem = pl.BlockSpec(memory_space=pltpu.VMEM)
    return pl.pallas_call(
        weight_kernel,
        out_shape=(
            jax.ShapeDtypeStruct((dates, rows, cols), jnp.float32),
            jax.ShapeDtypeStruct((rows, cols), jnp.float32),
        ),
        in_specs=[pl.BlockSpec(memory_space=pltpu.SMEM), vmem, vmem],
        out_specs=(vmem, vmem),
    )(class_score, scene_class, quality)


def inside_mask(row_start, col_start, height, width, total_rows, total_cols):
    rows = row_start + jnp.arange(height, dtype=jnp.int32)
    cols = col_start + jnp.arange(width, dtype=jnp.int32)
    row_in = (rows >= 0) & (rows < total_rows)
    col_in = (cols >= 0) & (cols < total_cols)
    return (row_in[:, None] & col_in[None, :])[:, :, None]


def masked_layer(field, kernel, row_start, col_start, total_rows, total_cols, conv=valid_conv):
    out = conv(field, kernel)
    mask = inside_mask(row_start, col_start, out.shape[0], out.shape[1], total_rows, total_cols)
    return jnp.where(mask, jnp.maximum(out, 0.0), 0.0).astype(jnp.bfloat16)


def shards(
    reflectance,
    scene_class,
    quality,
    class_score,
    encode_first,
    encode_second,
    middle_first,
    middle_second,
    decode_kernel,
    head_weight,
):
    block_rows = quality.shape[1]
    block_cols = quality.shape[2]
    total_rows = block_rows * lax.axis_size("row")
    total_cols = block_cols * lax.axis_size("col")
    weights, shift = shifted_weights(class_score, scene_class, quality)
    part_sums = jnp.sum(weights[:, None] * reflectance, axis=0)
    part_total = jnp.sum(weights, axis=0)
    packed = jnp.concatenate([part_sums, part_total[None], shift[None]], axis=0).astype(jnp.bfloat16)
    gathered = lax.all_gather(packed, "tm", axis=0).astype(jnp.float32)
    shifts = gathered[:, -1]
    scale = jnp.exp(shifts - jnp.max(shifts, axis=0)[None])
    band_sums = jnp.sum(scale[:, None] * gathered[:, :-2], axis=0)
    total_weight = jnp.sum(scale * gathered[:, -2], axis=0)
    composite = (band_sums / total_weight[None]).astype(jnp.bfloat16)

    row0 = lax.axis_index("row") * block_rows
    col0 = lax.axis_index("col") * block_cols
    tall = with_halo(composite, (("row", 1),), HALO).transpose(1, 2, 0)
    widened = with_halo(tall, (("col", 1),), HALO)
    first_map = masked_layer(widened, encode_first, row0 - HALO + 1, col0 - HALO + 1, total_rows, total_cols)
    skip_wide = masked_layer(first_map, encode_second, row0 - HALO + 2, col0 - HALO + 2, total_rows, total_cols)
    wide_rows, wide_cols, channels = skip_wide.shape
    col_pairs = jnp.einsum(
        "vw,hwc->hvc", pair_matrix(wide_cols // 2, wide_cols, 0), skip_wide, preferred_element_type=jnp.float32
    )
    pooled = (
        jnp.sum(col_pairs.reshape(wide_rows // 2, 2, wide_cols // 2, channels), axis=1) * 0.25
    ).astype(jnp.bfloat16)
    coarse_halo = (HALO - 2) // 2
    crow0 = row0 // 2 - coarse_halo
    ccol0 = col0 // 2 - coarse_halo
    coarse = (total_rows // 2, total_cols // 2, native_conv)
    mid = masked_layer(pooled, middle_first, crow0 + 1, ccol0 + 1, *coarse)
    deeper = masked_layer(mid, middle_second, crow0 + 2, ccol0 + 2, *coarse)
    up_halo = 2 * (coarse_halo - 2)
    deep_rows, deep_cols, deep_ch = deeper.shape
    spread = jnp.einsum(
        "wv,hvc->hwc",
        pair_matrix(deep_cols, block_cols + 2, up_halo - 1).T,
        deeper,
        preferred_element_type=jnp.float32,
    ).astype(jnp.bfloat16)
    upsampled = jnp.broadcast_to(spread[:, None], (deep_rows, 2, block_cols + 2, deep_ch)).reshape(
        2 * deep_rows, block_cols + 2, deep_ch
    )[up_halo - 1 : up_halo + block_rows + 1]
    skip_halo = HALO - 2
    skip = skip_wide[skip_halo - 1 : skip_halo + block_rows + 1, skip_halo - 1 : skip_halo + block_cols + 1]
    joined = jnp.concatenate([skip, upsampled], axis=2)
    decoded = jnp.maximum(valid_conv(joined, decode_kernel), 0.0).astype(jnp.bfloat16)
    return jnp.einsum(
        "oc,hwc->ohw", head_weight, decoded, preferred_element_type=jnp.float32
    ).astype(jnp.bfloat16)


def solution(mesh):
    placed = (
        P("tm", None, "row", "col"),
        P("tm", "row", "col"),
        P("tm", "row", "col"),
        P(),
        P(),
        P(),
        P(),
        P(),
        P(),
        P(),
    )
    return jax.shard_map(
        shards, mesh=mesh, in_specs=placed, out_specs=P(None, "row", "col"), check_vma=False
    )
```

```python
import jax
import jax.numpy as jnp
from jax import lax
from jax.experimental import pallas as pl
from jax.experimental.pallas import tpu as pltpu
from jax.sharding import PartitionSpec as P

HALO = 8


def with_halo(cells, sides, width):
    for axis, dim in sides:
        count = lax.axis_size(axis)
        ends = count - 1
        head = lax.slice_in_dim(cells, 0, width, axis=dim)
        tail = lax.slice_in_dim(cells, cells.shape[dim] - width, cells.shape[dim], axis=dim)
        if count == 2:
            first = lax.axis_index(axis) == 0
            got = lax.ppermute(jnp.where(first, tail, head), axis, [(0, 1), (1, 0)])
            empty = jnp.zeros_like(got)
            cells = jnp.concatenate(
                [jnp.where(first, empty, got), cells, jnp.where(first, got, empty)], axis=dim
            )
            continue
        cells = jnp.concatenate(
            [
                lax.ppermute(tail, axis, [(i, (i + 1) % count) for i in range(ends)]),
                cells,
                lax.ppermute(head, axis, [((i + 1) % count, i) for i in range(ends)]),
            ],
            axis=dim,
        )
    return cells


def valid_conv(padded, kernel):
    taps = kernel.shape[0]
    height = padded.shape[0] - taps + 1
    width = padded.shape[1] - taps + 1
    total = None
    for a in range(taps):
        for e in range(taps):
            term = jnp.einsum(
                "hwc,oc->hwo",
                padded[a : a + height, e : e + width],
                kernel[a, e],
                preferred_element_type=jnp.float32,
            )
            total = term if total is None else total + term
    return total


def native_conv(padded, kernel):
    return lax.conv_general_dilated(
        padded[None],
        kernel,
        (1, 1),
        "VALID",
        dimension_numbers=("NHWC", "HWOI", "NHWC"),
        preferred_element_type=jnp.float32,
    )[0]


def pair_matrix(narrow, wide, offset):
    pick = (jnp.arange(wide, dtype=jnp.int32) + offset) // 2
    return (jnp.arange(narrow, dtype=jnp.int32)[:, None] == pick[None, :]).astype(jnp.bfloat16)


def weight_kernel(score_ref, class_ref, quality_ref, weight_ref, shift_ref):
    dates, rows, _ = class_ref.shape
    classes = score_ref.shape[0]
    step = 16

    def chunk(index, carry):
        at = pl.ds(pl.multiple_of(index * step, step), step)

        def score(date, top):
            label = class_ref[date, at, :]
            looked = jnp.zeros(label.shape, jnp.float32)
            for k in range(classes):
                looked = jnp.where(label == k, score_ref[k], looked)
            value = looked + quality_ref[date, at, :]
            weight_ref[date, at, :] = value
            return jnp.maximum(top, value)

        start = jnp.full((step, weight_ref.shape[2]), -jnp.inf, jnp.float32)
        top = lax.fori_loop(0, dates, score, start)
        shift = top.astype(jnp.bfloat16).astype(jnp.float32)
        shift_ref[at, :] = shift

        def one_date(date, inner):
            weight_ref[date, at, :] = jnp.exp(weight_ref[date, at, :] - shift)
            return inner

        lax.fori_loop(0, dates, one_date, 0)
        return carry

    lax.fori_loop(0, rows // step, chunk, 0)


def shifted_weights(class_score, scene_class, quality):
    dates, rows, cols = quality.shape
    vmem = pl.BlockSpec(memory_space=pltpu.VMEM)
    return pl.pallas_call(
        weight_kernel,
        out_shape=(
            jax.ShapeDtypeStruct((dates, rows, cols), jnp.float32),
            jax.ShapeDtypeStruct((rows, cols), jnp.float32),
        ),
        in_specs=[pl.BlockSpec(memory_space=pltpu.SMEM), vmem, vmem],
        out_specs=(vmem, vmem),
    )(class_score, scene_class, quality)


def inside_mask(row_start, col_start, height, width, total_rows, total_cols):
    rows = row_start + jnp.arange(height, dtype=jnp.int32)
    cols = col_start + jnp.arange(width, dtype=jnp.int32)
    row_in = (rows >= 0) & (rows < total_rows)
    col_in = (cols >= 0) & (cols < total_cols)
    return (row_in[:, None] & col_in[None, :])[:, :, None]


def masked_layer(field, kernel, row_start, col_start, total_rows, total_cols, conv=valid_conv):
    out = conv(field, kernel)
    mask = inside_mask(row_start, col_start, out.shape[0], out.shape[1], total_rows, total_cols)
    return jnp.where(mask, jnp.maximum(out, 0.0), 0.0).astype(jnp.bfloat16)


def shards(
    reflectance,
    scene_class,
    quality,
    class_score,
    encode_first,
    encode_second,
    middle_first,
    middle_second,
    decode_kernel,
    head_weight,
):
    block_rows = quality.shape[1]
    block_cols = quality.shape[2]
    total_rows = block_rows * lax.axis_size("row")
    total_cols = block_cols * lax.axis_size("col")
    weights, shift = shifted_weights(class_score, scene_class, quality)
    part_sums = jnp.sum(weights[:, None] * reflectance, axis=0)
    part_total = jnp.sum(weights, axis=0)
    packed = jnp.concatenate([part_sums, part_total[None], shift[None]], axis=0).astype(jnp.bfloat16)
    gathered = lax.all_gather(packed, "tm", axis=0).astype(jnp.float32)
    shifts = gathered[:, -1]
    scale = jnp.exp(shifts - jnp.max(shifts, axis=0)[None])
    band_sums = jnp.sum(scale[:, None] * gathered[:, :-2], axis=0)
    total_weight = jnp.sum(scale * gathered[:, -2], axis=0)
    composite = (band_sums / total_weight[None]).astype(jnp.bfloat16)

    row0 = lax.axis_index("row") * block_rows
    col0 = lax.axis_index("col") * block_cols
    widened = with_halo(composite.transpose(1, 2, 0), (("row", 0), ("col", 1)), HALO)
    first_map = masked_layer(widened, encode_first, row0 - HALO + 1, col0 - HALO + 1, total_rows, total_cols)
    skip_wide = masked_layer(first_map, encode_second, row0 - HALO + 2, col0 - HALO + 2, total_rows, total_cols)
    wide_rows, wide_cols, channels = skip_wide.shape
    pooled = (
        jnp.einsum(
            "vw,hrwc->hvc",
            pair_matrix(wide_cols // 2, wide_cols, 0),
            skip_wide.reshape(wide_rows // 2, 2, wide_cols, channels),
            preferred_element_type=jnp.float32,
        )
        * 0.25
    ).astype(jnp.bfloat16)
    coarse_halo = (HALO - 2) // 2
    crow0 = row0 // 2 - coarse_halo
    ccol0 = col0 // 2 - coarse_halo
    coarse = (total_rows // 2, total_cols // 2, native_conv)
    mid = masked_layer(pooled, middle_first, crow0 + 1, ccol0 + 1, *coarse)
    deeper = masked_layer(mid, middle_second, crow0 + 2, ccol0 + 2, *coarse)
    up_halo = 2 * (coarse_halo - 2)
    deep_rows, deep_cols, deep_ch = deeper.shape
    spread = jnp.einsum(
        "wv,hvc->hwc",
        pair_matrix(deep_cols, block_cols + 2, up_halo - 1).T,
        deeper,
        preferred_element_type=jnp.float32,
    ).astype(jnp.bfloat16)
    upsampled = jnp.broadcast_to(spread[:, None], (deep_rows, 2, block_cols + 2, deep_ch)).reshape(
        2 * deep_rows, block_cols + 2, deep_ch
    )[up_halo - 1 : up_halo + block_rows + 1]
    skip_halo = HALO - 2
    skip = skip_wide[skip_halo - 1 : skip_halo + block_rows + 1, skip_halo - 1 : skip_halo + block_cols + 1]
    joined = jnp.concatenate([skip, upsampled], axis=2)
    decoded = jnp.maximum(valid_conv(joined, decode_kernel), 0.0).astype(jnp.bfloat16)
    return jnp.einsum(
        "oc,hwc->ohw", head_weight, decoded, preferred_element_type=jnp.float32
    ).astype(jnp.bfloat16)


def solution(mesh):
    placed = (
        P("tm", None, "row", "col"),
        P("tm", "row", "col"),
        P("tm", "row", "col"),
        P(),
        P(),
        P(),
        P(),
        P(),
        P(),
        P(),
    )
    return jax.shard_map(
        shards, mesh=mesh, in_specs=placed, out_specs=P(None, "row", "col"), check_vma=False
    )
```

```python
import jax
import jax.numpy as jnp
from jax import lax
from jax.experimental import pallas as pl
from jax.experimental.pallas import tpu as pltpu
from jax.sharding import PartitionSpec as P

HALO = 8


def with_halo(cells, sides, width):
    for axis, dim in sides:
        count = lax.axis_size(axis)
        ends = count - 1
        head = lax.slice_in_dim(cells, 0, width, axis=dim)
        tail = lax.slice_in_dim(cells, cells.shape[dim] - width, cells.shape[dim], axis=dim)
        if count == 2:
            first = lax.axis_index(axis) == 0
            got = lax.ppermute(jnp.where(first, tail, head), axis, [(0, 1), (1, 0)])
            empty = jnp.zeros_like(got)
            cells = jnp.concatenate(
                [jnp.where(first, empty, got), cells, jnp.where(first, got, empty)], axis=dim
            )
            continue
        cells = jnp.concatenate(
            [
                lax.ppermute(tail, axis, [(i, (i + 1) % count) for i in range(ends)]),
                cells,
                lax.ppermute(head, axis, [((i + 1) % count, i) for i in range(ends)]),
            ],
            axis=dim,
        )
    return cells


def valid_conv(padded, kernel):
    taps = kernel.shape[0]
    height = padded.shape[0] - taps + 1
    width = padded.shape[1] - taps + 1
    total = None
    for a in range(taps):
        for e in range(taps):
            term = jnp.einsum(
                "hwc,oc->hwo",
                padded[a : a + height, e : e + width],
                kernel[a, e],
                preferred_element_type=jnp.float32,
            )
            total = term if total is None else total + term
    return total


def native_conv(padded, kernel):
    return lax.conv_general_dilated(
        padded[None],
        kernel,
        (1, 1),
        "VALID",
        dimension_numbers=("NHWC", "HWOI", "NHWC"),
        preferred_element_type=jnp.float32,
    )[0]


def pair_matrix(narrow, wide, offset):
    pick = (jnp.arange(wide, dtype=jnp.int32) + offset) // 2
    return (jnp.arange(narrow, dtype=jnp.int32)[:, None] == pick[None, :]).astype(jnp.bfloat16)


def weight_kernel(score_ref, class_ref, quality_ref, weight_ref, shift_ref, value_ref):
    dates, rows, _ = class_ref.shape
    classes = score_ref.shape[0]
    step = value_ref.shape[1]

    def chunk(index, carry):
        at = pl.ds(pl.multiple_of(index * step, step), step)

        def score(date, top):
            label = class_ref[date, at, :]
            looked = jnp.zeros(label.shape, jnp.float32)
            for k in range(classes):
                looked = jnp.where(label == k, score_ref[k], looked)
            value = looked + quality_ref[date, at, :]
            value_ref[date] = value
            return jnp.maximum(top, value)

        start = jnp.full((step, value_ref.shape[2]), -jnp.inf, jnp.float32)
        top = lax.fori_loop(0, dates, score, start)
        shift = top.astype(jnp.bfloat16).astype(jnp.float32)
        shift_ref[at, :] = shift

        def one_date(date, inner):
            weight_ref[date, at, :] = jnp.exp(value_ref[date] - shift).astype(weight_ref.dtype)
            return inner

        lax.fori_loop(0, dates, one_date, 0)
        return carry

    lax.fori_loop(0, rows // step, chunk, 0)


def shifted_weights(class_score, scene_class, quality):
    dates, rows, cols = quality.shape
    vmem = pl.BlockSpec(memory_space=pltpu.VMEM)
    return pl.pallas_call(
        weight_kernel,
        out_shape=(
            jax.ShapeDtypeStruct((dates, rows, cols), jnp.bfloat16),
            jax.ShapeDtypeStruct((rows, cols), jnp.float32),
        ),
        in_specs=[pl.BlockSpec(memory_space=pltpu.SMEM), vmem, vmem],
        out_specs=(vmem, vmem),
        scratch_shapes=[pltpu.VMEM((dates, 16, cols), jnp.float32)],
    )(class_score, scene_class, quality)


def inside_mask(row_start, col_start, height, width, total_rows, total_cols):
    rows = row_start + jnp.arange(height, dtype=jnp.int32)
    cols = col_start + jnp.arange(width, dtype=jnp.int32)
    row_in = (rows >= 0) & (rows < total_rows)
    col_in = (cols >= 0) & (cols < total_cols)
    return (row_in[:, None] & col_in[None, :])[:, :, None]


def masked_layer(field, kernel, row_start, col_start, total_rows, total_cols, conv=valid_conv):
    out = conv(field, kernel)
    mask = inside_mask(row_start, col_start, out.shape[0], out.shape[1], total_rows, total_cols)
    return jnp.where(mask, jnp.maximum(out, 0.0), 0.0).astype(jnp.bfloat16)


def shards(
    reflectance,
    scene_class,
    quality,
    class_score,
    encode_first,
    encode_second,
    middle_first,
    middle_second,
    decode_kernel,
    head_weight,
):
    block_rows = quality.shape[1]
    block_cols = quality.shape[2]
    total_rows = block_rows * lax.axis_size("row")
    total_cols = block_cols * lax.axis_size("col")
    weights, shift = shifted_weights(class_score, scene_class, quality)
    weights = weights.astype(jnp.float32)
    part_sums = jnp.sum(weights[:, None] * reflectance.astype(jnp.float32), axis=0)
    part_total = jnp.sum(weights, axis=0)
    packed = jnp.concatenate([part_sums, part_total[None], shift[None]], axis=0).astype(jnp.bfloat16)
    gathered = lax.all_gather(packed, "tm", axis=0).astype(jnp.float32)
    shifts = gathered[:, -1]
    scale = jnp.exp(shifts - jnp.max(shifts, axis=0)[None])
    band_sums = jnp.sum(scale[:, None] * gathered[:, :-2], axis=0)
    total_weight = jnp.sum(scale * gathered[:, -2], axis=0)
    composite = (band_sums / total_weight[None]).astype(jnp.bfloat16)

    row0 = lax.axis_index("row") * block_rows
    col0 = lax.axis_index("col") * block_cols
    widened = with_halo(composite.transpose(1, 2, 0), (("row", 0), ("col", 1)), HALO)
    first_map = masked_layer(widened, encode_first, row0 - HALO + 1, col0 - HALO + 1, total_rows, total_cols)
    skip_wide = masked_layer(first_map, encode_second, row0 - HALO + 2, col0 - HALO + 2, total_rows, total_cols)
    wide_rows, wide_cols, channels = skip_wide.shape
    pooled = (
        jnp.einsum(
            "vw,hrwc->hvc",
            pair_matrix(wide_cols // 2, wide_cols, 0),
            skip_wide.reshape(wide_rows // 2, 2, wide_cols, channels),
            preferred_element_type=jnp.float32,
        )
        * 0.25
    ).astype(jnp.bfloat16)
    coarse_halo = (HALO - 2) // 2
    crow0 = row0 // 2 - coarse_halo
    ccol0 = col0 // 2 - coarse_halo
    coarse = (total_rows // 2, total_cols // 2, native_conv)
    mid = masked_layer(pooled, middle_first, crow0 + 1, ccol0 + 1, *coarse)
    deeper = masked_layer(mid, middle_second, crow0 + 2, ccol0 + 2, *coarse)
    up_halo = 2 * (coarse_halo - 2)
    deep_rows, deep_cols, deep_ch = deeper.shape
    spread = jnp.einsum(
        "wv,hvc->hwc",
        pair_matrix(deep_cols, block_cols + 2, up_halo - 1).T,
        deeper,
        preferred_element_type=jnp.float32,
    ).astype(jnp.bfloat16)
    upsampled = jnp.broadcast_to(spread[:, None], (deep_rows, 2, block_cols + 2, deep_ch)).reshape(
        2 * deep_rows, block_cols + 2, deep_ch
    )[up_halo - 1 : up_halo + block_rows + 1]
    skip_halo = HALO - 2
    skip = skip_wide[skip_halo - 1 : skip_halo + block_rows + 1, skip_halo - 1 : skip_halo + block_cols + 1]
    joined = jnp.concatenate([skip, upsampled], axis=2)
    decoded = jnp.maximum(valid_conv(joined, decode_kernel), 0.0).astype(jnp.bfloat16)
    return jnp.einsum(
        "oc,hwc->ohw", head_weight, decoded, preferred_element_type=jnp.float32
    ).astype(jnp.bfloat16)


def solution(mesh):
    placed = (
        P("tm", None, "row", "col"),
        P("tm", "row", "col"),
        P("tm", "row", "col"),
        P(),
        P(),
        P(),
        P(),
        P(),
        P(),
        P(),
    )
    return jax.shard_map(
        shards, mesh=mesh, in_specs=placed, out_specs=P(None, "row", "col"), check_vma=False
    )
```

```python
import jax
import jax.numpy as jnp
from jax import lax
from jax.experimental import pallas as pl
from jax.experimental.pallas import tpu as pltpu
from jax.sharding import PartitionSpec as P

HALO = 8


def with_halo(cells, sides, width):
    for axis, dim in sides:
        count = lax.axis_size(axis)
        ends = count - 1
        head = lax.slice_in_dim(cells, 0, width, axis=dim)
        tail = lax.slice_in_dim(cells, cells.shape[dim] - width, cells.shape[dim], axis=dim)
        if count == 2:
            first = lax.axis_index(axis) == 0
            got = lax.ppermute(jnp.where(first, tail, head), axis, [(0, 1), (1, 0)])
            empty = jnp.zeros_like(got)
            cells = jnp.concatenate(
                [jnp.where(first, empty, got), cells, jnp.where(first, got, empty)], axis=dim
            )
            continue
        cells = jnp.concatenate(
            [
                lax.ppermute(tail, axis, [(i, (i + 1) % count) for i in range(ends)]),
                cells,
                lax.ppermute(head, axis, [((i + 1) % count, i) for i in range(ends)]),
            ],
            axis=dim,
        )
    return cells


def valid_conv(padded, kernel):
    taps = kernel.shape[0]
    height = padded.shape[0] - taps + 1
    width = padded.shape[1] - taps + 1
    total = None
    for a in range(taps):
        for e in range(taps):
            term = jnp.einsum(
                "hwc,oc->hwo",
                padded[a : a + height, e : e + width],
                kernel[a, e],
                preferred_element_type=jnp.float32,
            )
            total = term if total is None else total + term
    return total


def native_conv(padded, kernel):
    return lax.conv_general_dilated(
        padded[None],
        kernel,
        (1, 1),
        "VALID",
        dimension_numbers=("NHWC", "HWOI", "NHWC"),
        preferred_element_type=jnp.float32,
    )[0]


def pair_matrix(narrow, wide, offset):
    pick = (jnp.arange(wide, dtype=jnp.int32) + offset) // 2
    return (jnp.arange(narrow, dtype=jnp.int32)[:, None] == pick[None, :]).astype(jnp.bfloat16)


def weight_kernel(score_ref, class_ref, quality_ref, weight_ref, shift_ref):
    dates, rows, _ = class_ref.shape
    classes = score_ref.shape[0]
    step = 16

    def chunk(index, carry):
        at = pl.ds(pl.multiple_of(index * step, step), step)

        def score(date, top):
            label = class_ref[date, at, :]
            options = [score_ref[k] for k in range(classes)]
            level = 0
            while len(options) > 1:
                bit = (label & (1 << level)) != 0
                options = [
                    jnp.where(bit, options[j + 1], options[j]) if j + 1 < len(options) else options[j]
                    for j in range(0, len(options), 2)
                ]
                level += 1
            value = options[0] + quality_ref[date, at, :]
            weight_ref[date, at, :] = value
            return jnp.maximum(top, value)

        start = jnp.full((step, weight_ref.shape[2]), -jnp.inf, jnp.float32)
        top = lax.fori_loop(0, dates, score, start)
        shift = top.astype(jnp.bfloat16).astype(jnp.float32)
        shift_ref[at, :] = shift

        def one_date(date, inner):
            weight_ref[date, at, :] = jnp.exp(weight_ref[date, at, :] - shift)
            return inner

        lax.fori_loop(0, dates, one_date, 0)
        return carry

    lax.fori_loop(0, rows // step, chunk, 0)


def shifted_weights(class_score, scene_class, quality):
    dates, rows, cols = quality.shape
    vmem = pl.BlockSpec(memory_space=pltpu.VMEM)
    return pl.pallas_call(
        weight_kernel,
        out_shape=(
            jax.ShapeDtypeStruct((dates, rows, cols), jnp.float32),
            jax.ShapeDtypeStruct((rows, cols), jnp.float32),
        ),
        in_specs=[pl.BlockSpec(memory_space=pltpu.SMEM), vmem, vmem],
        out_specs=(vmem, vmem),
    )(class_score, scene_class, quality)


def inside_mask(row_start, col_start, height, width, total_rows, total_cols):
    rows = row_start + jnp.arange(height, dtype=jnp.int32)
    cols = col_start + jnp.arange(width, dtype=jnp.int32)
    row_in = (rows >= 0) & (rows < total_rows)
    col_in = (cols >= 0) & (cols < total_cols)
    return (row_in[:, None] & col_in[None, :])[:, :, None]


def masked_layer(field, kernel, row_start, col_start, total_rows, total_cols, conv=valid_conv):
    out = conv(field, kernel)
    mask = inside_mask(row_start, col_start, out.shape[0], out.shape[1], total_rows, total_cols)
    return jnp.where(mask, jnp.maximum(out, 0.0), 0.0).astype(jnp.bfloat16)


def shards(
    reflectance,
    scene_class,
    quality,
    class_score,
    encode_first,
    encode_second,
    middle_first,
    middle_second,
    decode_kernel,
    head_weight,
):
    block_rows = quality.shape[1]
    block_cols = quality.shape[2]
    total_rows = block_rows * lax.axis_size("row")
    total_cols = block_cols * lax.axis_size("col")
    weights, shift = shifted_weights(class_score, scene_class, quality)
    part_sums = jnp.sum(weights[:, None] * reflectance, axis=0)
    part_total = jnp.sum(weights, axis=0)
    packed = jnp.concatenate([part_sums, part_total[None], shift[None]], axis=0).astype(jnp.bfloat16)
    gathered = lax.all_gather(packed, "tm", axis=0).astype(jnp.float32)
    shifts = gathered[:, -1]
    scale = jnp.exp(shifts - jnp.max(shifts, axis=0)[None])
    band_sums = jnp.sum(scale[:, None] * gathered[:, :-2], axis=0)
    total_weight = jnp.sum(scale * gathered[:, -2], axis=0)
    composite = (band_sums / total_weight[None]).astype(jnp.bfloat16)

    row0 = lax.axis_index("row") * block_rows
    col0 = lax.axis_index("col") * block_cols
    widened = with_halo(composite.transpose(1, 2, 0), (("row", 0), ("col", 1)), HALO)
    first_map = masked_layer(widened, encode_first, row0 - HALO + 1, col0 - HALO + 1, total_rows, total_cols)
    skip_wide = masked_layer(first_map, encode_second, row0 - HALO + 2, col0 - HALO + 2, total_rows, total_cols)
    wide_rows, wide_cols, channels = skip_wide.shape
    pooled = (
        jnp.einsum(
            "vw,hrwc->hvc",
            pair_matrix(wide_cols // 2, wide_cols, 0),
            skip_wide.reshape(wide_rows // 2, 2, wide_cols, channels),
            preferred_element_type=jnp.float32,
        )
        * 0.25
    ).astype(jnp.bfloat16)
    coarse_halo = (HALO - 2) // 2
    crow0 = row0 // 2 - coarse_halo
    ccol0 = col0 // 2 - coarse_halo
    coarse = (total_rows // 2, total_cols // 2, native_conv)
    mid = masked_layer(pooled, middle_first, crow0 + 1, ccol0 + 1, *coarse)
    deeper = masked_layer(mid, middle_second, crow0 + 2, ccol0 + 2, *coarse)
    up_halo = 2 * (coarse_halo - 2)
    deep_rows, deep_cols, deep_ch = deeper.shape
    spread = jnp.einsum(
        "wv,hvc->hwc",
        pair_matrix(deep_cols, block_cols + 2, up_halo - 1).T,
        deeper,
        preferred_element_type=jnp.float32,
    ).astype(jnp.bfloat16)
    upsampled = jnp.broadcast_to(spread[:, None], (deep_rows, 2, block_cols + 2, deep_ch)).reshape(
        2 * deep_rows, block_cols + 2, deep_ch
    )[up_halo - 1 : up_halo + block_rows + 1]
    skip_halo = HALO - 2
    skip = skip_wide[skip_halo - 1 : skip_halo + block_rows + 1, skip_halo - 1 : skip_halo + block_cols + 1]
    joined = jnp.concatenate([skip, upsampled], axis=2)
    decoded = jnp.maximum(valid_conv(joined, decode_kernel), 0.0).astype(jnp.bfloat16)
    return jnp.einsum(
        "oc,hwc->ohw", head_weight, decoded, preferred_element_type=jnp.float32
    ).astype(jnp.bfloat16)


def solution(mesh):
    placed = (
        P("tm", None, "row", "col"),
        P("tm", "row", "col"),
        P("tm", "row", "col"),
        P(),
        P(),
        P(),
        P(),
        P(),
        P(),
        P(),
    )
    return jax.shard_map(
        shards, mesh=mesh, in_specs=placed, out_specs=P(None, "row", "col"), check_vma=False
    )
```

```python
import jax
import jax.numpy as jnp
from jax import lax
from jax.experimental import pallas as pl
from jax.experimental.pallas import tpu as pltpu
from jax.sharding import PartitionSpec as P

HALO = 8


def with_halo(cells, sides, width):
    for axis, dim in sides:
        count = lax.axis_size(axis)
        ends = count - 1
        head = lax.slice_in_dim(cells, 0, width, axis=dim)
        tail = lax.slice_in_dim(cells, cells.shape[dim] - width, cells.shape[dim], axis=dim)
        if count == 2:
            first = lax.axis_index(axis) == 0
            got = lax.ppermute(jnp.where(first, tail, head), axis, [(0, 1), (1, 0)])
            empty = jnp.zeros_like(got)
            cells = jnp.concatenate(
                [jnp.where(first, empty, got), cells, jnp.where(first, got, empty)], axis=dim
            )
            continue
        cells = jnp.concatenate(
            [
                lax.ppermute(tail, axis, [(i, (i + 1) % count) for i in range(ends)]),
                cells,
                lax.ppermute(head, axis, [((i + 1) % count, i) for i in range(ends)]),
            ],
            axis=dim,
        )
    return cells


def valid_conv(padded, kernel):
    taps = kernel.shape[0]
    height = padded.shape[0] - taps + 1
    width = padded.shape[1] - taps + 1
    total = None
    for a in range(taps):
        for e in range(taps):
            term = jnp.einsum(
                "hwc,oc->hwo",
                padded[a : a + height, e : e + width],
                kernel[a, e],
                preferred_element_type=jnp.float32,
            )
            total = term if total is None else total + term
    return total


def native_conv(padded, kernel):
    return lax.conv_general_dilated(
        padded[None],
        kernel,
        (1, 1),
        "VALID",
        dimension_numbers=("NHWC", "HWOI", "NHWC"),
        preferred_element_type=jnp.float32,
    )[0]


def pair_matrix(narrow, wide, offset):
    pick = (jnp.arange(wide, dtype=jnp.int32) + offset) // 2
    return (jnp.arange(narrow, dtype=jnp.int32)[:, None] == pick[None, :]).astype(jnp.bfloat16)


def weight_kernel(score_ref, class_ref, quality_ref, weight_ref, shift_ref):
    dates, rows, _ = class_ref.shape
    classes = score_ref.shape[0]
    step = 32 if rows % 32 == 0 else 16

    def chunk(index, carry):
        at = pl.ds(pl.multiple_of(index * step, step), step)

        def score(date, top):
            label = class_ref[date, at, :]
            options = [score_ref[k] for k in range(classes)]
            level = 0
            while len(options) > 1:
                bit = (label & (1 << level)) != 0
                options = [
                    jnp.where(bit, options[j + 1], options[j]) if j + 1 < len(options) else options[j]
                    for j in range(0, len(options), 2)
                ]
                level += 1
            value = options[0] + quality_ref[date, at, :]
            weight_ref[date, at, :] = value
            return jnp.maximum(top, value)

        start = jnp.full((step, weight_ref.shape[2]), -jnp.inf, jnp.float32)
        top = lax.fori_loop(0, dates, score, start)
        shift = top.astype(jnp.bfloat16).astype(jnp.float32)
        shift_ref[at, :] = shift

        def one_date(date, inner):
            weight_ref[date, at, :] = jnp.exp(weight_ref[date, at, :] - shift)
            return inner

        lax.fori_loop(0, dates, one_date, 0)
        return carry

    lax.fori_loop(0, rows // step, chunk, 0)


def shifted_weights(class_score, scene_class, quality):
    dates, rows, cols = quality.shape
    vmem = pl.BlockSpec(memory_space=pltpu.VMEM)
    return pl.pallas_call(
        weight_kernel,
        out_shape=(
            jax.ShapeDtypeStruct((dates, rows, cols), jnp.float32),
            jax.ShapeDtypeStruct((rows, cols), jnp.float32),
        ),
        in_specs=[pl.BlockSpec(memory_space=pltpu.SMEM), vmem, vmem],
        out_specs=(vmem, vmem),
    )(class_score, scene_class, quality)


def inside_mask(row_start, col_start, height, width, total_rows, total_cols):
    rows = row_start + jnp.arange(height, dtype=jnp.int32)
    cols = col_start + jnp.arange(width, dtype=jnp.int32)
    row_in = (rows >= 0) & (rows < total_rows)
    col_in = (cols >= 0) & (cols < total_cols)
    return (row_in[:, None] & col_in[None, :])[:, :, None]


def masked_layer(field, kernel, row_start, col_start, total_rows, total_cols, conv=valid_conv):
    out = conv(field, kernel)
    mask = inside_mask(row_start, col_start, out.shape[0], out.shape[1], total_rows, total_cols)
    return jnp.where(mask, jnp.maximum(out, 0.0), 0.0).astype(jnp.bfloat16)


def shards(
    reflectance,
    scene_class,
    quality,
    class_score,
    encode_first,
    encode_second,
    middle_first,
    middle_second,
    decode_kernel,
    head_weight,
):
    block_rows = quality.shape[1]
    block_cols = quality.shape[2]
    total_rows = block_rows * lax.axis_size("row")
    total_cols = block_cols * lax.axis_size("col")
    weights, shift = shifted_weights(class_score, scene_class, quality)
    part_sums = jnp.sum(weights[:, None] * reflectance, axis=0)
    part_total = jnp.sum(weights, axis=0)
    packed = jnp.concatenate([part_sums, part_total[None], shift[None]], axis=0).astype(jnp.bfloat16)
    gathered = lax.all_gather(packed, "tm", axis=0).astype(jnp.float32)
    shifts = gathered[:, -1]
    scale = jnp.exp(shifts - jnp.max(shifts, axis=0)[None])
    band_sums = jnp.sum(scale[:, None] * gathered[:, :-2], axis=0)
    total_weight = jnp.sum(scale * gathered[:, -2], axis=0)
    composite = (band_sums / total_weight[None]).astype(jnp.bfloat16)

    row0 = lax.axis_index("row") * block_rows
    col0 = lax.axis_index("col") * block_cols
    widened = with_halo(composite.transpose(1, 2, 0), (("row", 0), ("col", 1)), HALO)
    first_map = masked_layer(widened, encode_first, row0 - HALO + 1, col0 - HALO + 1, total_rows, total_cols)
    skip_wide = masked_layer(first_map, encode_second, row0 - HALO + 2, col0 - HALO + 2, total_rows, total_cols)
    wide_rows, wide_cols, channels = skip_wide.shape
    pooled = (
        jnp.einsum(
            "vw,hrwc->hvc",
            pair_matrix(wide_cols // 2, wide_cols, 0),
            skip_wide.reshape(wide_rows // 2, 2, wide_cols, channels),
            preferred_element_type=jnp.float32,
        )
        * 0.25
    ).astype(jnp.bfloat16)
    coarse_halo = (HALO - 2) // 2
    crow0 = row0 // 2 - coarse_halo
    ccol0 = col0 // 2 - coarse_halo
    coarse = (total_rows // 2, total_cols // 2, native_conv)
    mid = masked_layer(pooled, middle_first, crow0 + 1, ccol0 + 1, *coarse)
    deeper = masked_layer(mid, middle_second, crow0 + 2, ccol0 + 2, *coarse)
    up_halo = 2 * (coarse_halo - 2)
    deep_rows, deep_cols, deep_ch = deeper.shape
    spread = jnp.einsum(
        "wv,hvc->hwc",
        pair_matrix(deep_cols, block_cols + 2, up_halo - 1).T,
        deeper,
        preferred_element_type=jnp.float32,
    ).astype(jnp.bfloat16)
    upsampled = jnp.broadcast_to(spread[:, None], (deep_rows, 2, block_cols + 2, deep_ch)).reshape(
        2 * deep_rows, block_cols + 2, deep_ch
    )[up_halo - 1 : up_halo + block_rows + 1]
    skip_halo = HALO - 2
    skip = skip_wide[skip_halo - 1 : skip_halo + block_rows + 1, skip_halo - 1 : skip_halo + block_cols + 1]
    joined = jnp.concatenate([skip, upsampled], axis=2)
    decoded = jnp.maximum(valid_conv(joined, decode_kernel), 0.0).astype(jnp.bfloat16)
    return jnp.einsum(
        "oc,hwc->ohw", head_weight, decoded, preferred_element_type=jnp.float32
    ).astype(jnp.bfloat16)


def solution(mesh):
    placed = (
        P("tm", None, "row", "col"),
        P("tm", "row", "col"),
        P("tm", "row", "col"),
        P(),
        P(),
        P(),
        P(),
        P(),
        P(),
        P(),
    )
    return jax.shard_map(
        shards, mesh=mesh, in_specs=placed, out_specs=P(None, "row", "col"), check_vma=False
    )
```
